128 devices in a mesh: pipe: 2 (over x_hi), tensor: 4 (over x_lo, core), dp: 16 (over z, y).
Axes of the slice: x: 4 (x_hi: 2, x_lo: 2; x = x_hi * 2 + x_lo), y: 4, z: 4, core: 2. Of those that a mesh axis runs over, the one named last changes fastest.
Arguments:
- tokens: bfloat16 [16, 128, 4096], P('dp'), may hold values from -600 to 600
- norm_gains: float32 [2, 4096], P('pipe'), may hold values from 0.5 to 1.5
- qkv_weight: bfloat16 [2, 4096, 6144], P('pipe', 'dp', 'tensor'), may hold values from -0.1875 to 0.1875
- out_weight: bfloat16 [2, 4096, 4096], P('pipe', 'dp', 'tensor'), may hold values from -0.09375 to 0.09375
- cotangent: bfloat16 [16, 128, 4096], P('dp'), may hold values from -1.25 to 1.25
Outputs:
- qkv_grad: float32 [2, 4096, 6144], P('pipe', 'dp', 'tensor')
- out_grad: float32 [2, 4096, 4096], P('pipe', 'dp', 'tensor')
- gain_grad: float32 [2, 4096], P('pipe', 'dp')
The draws below stay inside these ranges and needn't reach their ends.
All inputs are finite; a program needn't handle non-finite values.
Results may differ from the reference program's by a relative error of at most 0.025.
Values may be sent and summed in bfloat16 or wider, within the bound.
No kernel may reach another device: no remote copies, remote signals or barrier semaphores. Data moves between devices by JAX's collectives and lax.ppermute only.
A program may use at most 128 MiB of HBM per device.

```python
import jax
import jax.numpy as jnp
from jax import lax

D = 4096
HD = 128
KVH = 8
GROUP = 4
SEQ = 128
LAYERS = 2
SEQS = 16


def draw_tokens(key, part):
    values = jnp.clip(jax.random.normal(jax.random.fold_in(key, 11), (SEQS, SEQ, D), jnp.float32), -6.0, 6.0)
    return values.astype(jnp.bfloat16)


def draw_qkv_weight(key, part):
    columns = KVH * (GROUP + 2) * HD
    values = jnp.clip(jax.random.normal(jax.random.fold_in(key, 21), (LAYERS, D, columns), jnp.float32), -6.0, 6.0) * D ** (-0.5)
    return values.astype(jnp.bfloat16)


def steps_of(key, dims, shards, low, top_value):
    gain, own = 1.0, jax.random.fold_in(key, 6)
    for axis_at, blocks in shards:
        steps = jnp.exp(jax.random.uniform(jax.random.fold_in(own, axis_at), (blocks,), jnp.float32, low / len(shards), top_value / len(shards)))
        gain = gain * jnp.repeat(steps, dims[axis_at] // blocks).reshape([-1 if axis == axis_at else 1 for axis in range(len(dims))])
    return gain


def centred(key, dims, spread, bound, shards=(), dtype=jnp.bfloat16):
    gain = steps_of(key, dims, shards, -0.22, 0.18) if shards else 1.0
    drawn = jax.random.normal(key, dims, jnp.float32) * spread * gain
    return jnp.minimum(jnp.maximum(drawn, -bound), bound).astype(dtype)


def setup_inputs(seed: int = 0) -> dict:
    key_list = jax.random.split(jax.random.key(seed), 6)
    return {
        "tokens": draw_tokens(jax.random.fold_in(key_list[5], 71), 0),
        "norm_gains": jnp.clip(1.0 + 0.1 * jax.random.normal(key_list[1], (LAYERS, D), jnp.float32), 0.5, 1.5),
        "qkv_weight": draw_qkv_weight(jax.random.fold_in(key_list[5], 71), 0),
        "out_weight": centred(key_list[3], (LAYERS, D, KVH * GROUP * HD), (KVH * GROUP * HD) ** -0.5, 0.09375, ((0, 2), (1, 16), (2, 4))),
        "cotangent": centred(key_list[4], (SEQS, SEQ, D), (4.0 / (SEQ * SEQS) ** 0.5), 1.25, ((0, 16),)),
    }


EPSILON = 1e-05
HIGH = lax.Precision.HIGHEST

def norm_parts(block_rows, gain_row):
    values = block_rows.astype(jnp.float32)
    recip_rms = lax.rsqrt(lax.optimization_barrier(jnp.mean(values * values, axis=-1, keepdims=True)) + EPSILON)
    normed = values * recip_rms
    return (normed, recip_rms, (normed * gain_row.astype(jnp.float32)).astype(jnp.bfloat16))

def attend(query_rows, key_rows, value_rows, query_pos, key_pos):
    score_scale = HD ** (-0.5)
    scores = jnp.einsum('rgjd,cgd->gjrc', query_rows.astype(jnp.float32), key_rows.astype(jnp.float32), precision=HIGH) * score_scale
    allowed = key_pos[None, :] <= query_pos[:, None]
    scores = jnp.where(allowed, scores, -jnp.inf)
    row_max = lax.optimization_barrier(jnp.max(scores, axis=-1, keepdims=True))
    raised = jnp.exp(scores - row_max)
    attn_probs = raised / lax.optimization_barrier(jnp.sum(raised, axis=-1, keepdims=True))
    probs_low = attn_probs.astype(jnp.bfloat16)
    mixed_rows = jnp.einsum('gjrc,cgd->rgjd', lax.optimization_barrier(probs_low).astype(jnp.float32), value_rows.astype(jnp.float32), precision=HIGH)
    return (attn_probs, probs_low, mixed_rows.astype(jnp.bfloat16))

def attend_back(query_rows, key_rows, value_rows, attn_probs, probs_low, grad_mixed):
    score_scale = HD ** (-0.5)
    grad_float = grad_mixed.astype(jnp.float32)
    grad_low = jnp.einsum('rgjd,cgd->gjrc', grad_float, value_rows.astype(jnp.float32), precision=HIGH)
    inner_sum = lax.optimization_barrier(jnp.sum(attn_probs * grad_low, axis=-1, keepdims=True))
    grad_score = attn_probs * (grad_low - inner_sum) * score_scale
    grad_query = jnp.einsum('gjrc,cgd->rgjd', grad_score, key_rows.astype(jnp.float32), precision=HIGH)
    grad_key = jnp.einsum('gjrc,rgjd->cgd', grad_score, query_rows.astype(jnp.float32), precision=HIGH)
    grad_value = jnp.einsum('gjrc,rgjd->cgd', probs_low.astype(jnp.float32), grad_float, precision=HIGH)
    return (grad_query, grad_key, grad_value)

def layer_forward(layer_in, gain_row, qkv_mat, out_mat):
    normed, recip_rms, normed_low = norm_parts(layer_in, gain_row)
    projected = jnp.dot(normed_low, qkv_mat, preferred_element_type=jnp.float32).reshape(SEQ, KVH, GROUP + 2, HD)
    query_rows = projected[:, :, :GROUP].astype(jnp.bfloat16)
    key_rows = projected[:, :, GROUP].astype(jnp.bfloat16)
    value_rows = projected[:, :, GROUP + 1].astype(jnp.bfloat16)
    positions = jnp.arange(SEQ)
    attn_probs, probs_low, mixed_rows = attend(query_rows, key_rows, value_rows, positions, positions)
    flat_mixed = mixed_rows.reshape(SEQ, KVH * GROUP * HD)
    summed = lax.dot_general(flat_mixed, out_mat, (((1,), (1,)), ((), ())), preferred_element_type=jnp.float32)
    layer_out = (layer_in.astype(jnp.float32) + summed).astype(jnp.bfloat16)
    return (layer_out, (normed, recip_rms, normed_low, query_rows, key_rows, value_rows, attn_probs, probs_low, flat_mixed))

def layer_backward(grad_out, gain_row, qkv_mat, out_mat, saved):
    normed, recip_rms, normed_low, query_rows, key_rows, value_rows, attn_probs, probs_low, flat_mixed = saved
    grad_mixed = jnp.dot(grad_out, out_mat, preferred_element_type=jnp.float32).astype(jnp.bfloat16).reshape(SEQ, KVH, GROUP, HD)
    grad_query, grad_key, grad_value = attend_back(query_rows, key_rows, value_rows, attn_probs, probs_low, grad_mixed)
    grad_proj = jnp.concatenate([grad_query.astype(jnp.bfloat16), grad_key.astype(jnp.bfloat16)[:, :, None], grad_value.astype(jnp.bfloat16)[:, :, None]], axis=2).reshape(SEQ, KVH * (GROUP + 2) * HD)
    grad_normed = lax.dot_general(grad_proj, qkv_mat, (((1,), (1,)), ((), ())), preferred_element_type=jnp.float32).astype(jnp.bfloat16)
    grad_float = grad_normed.astype(jnp.float32)
    scaled = grad_float * gain_row.astype(jnp.float32)
    grad_norm_in = recip_rms * (scaled - normed * lax.optimization_barrier(jnp.mean(scaled * normed, axis=-1, keepdims=True)))
    grad_in = (grad_out.astype(jnp.float32) + grad_norm_in).astype(jnp.bfloat16)
    part_qkv = lax.dot_general(normed_low, grad_proj, (((0,), (0,)), ((), ())), preferred_element_type=jnp.float32)
    part_out = lax.dot_general(grad_out, flat_mixed, (((0,), (0,)), ((), ())), preferred_element_type=jnp.float32)
    part_gain = lax.optimization_barrier(jnp.sum(grad_float * normed, axis=0))
    return (grad_in, part_qkv, part_out, part_gain)

def merge_parts(parts):
    return lax.optimization_barrier(jnp.sum(lax.optimization_barrier(parts.astype(jnp.bfloat16)).astype(jnp.float32), axis=0))

def reference(tokens, norm_gains, qkv_weight, out_weight, cotangent):
    forward = jax.vmap(layer_forward, in_axes=(0, None, None, None))
    backward = jax.vmap(layer_backward, in_axes=(0, None, None, None, 0))
    hidden_rows = tokens
    saved_layers = []
    for layer_index in range(LAYERS):
        hidden_rows, saved = forward(hidden_rows, norm_gains[layer_index], qkv_weight[layer_index], out_weight[layer_index])
        saved_layers.append(saved)
    flowing = cotangent
    qkv_list = [None] * LAYERS
    out_list = [None] * LAYERS
    gain_list = [None] * LAYERS
    for layer_index in reversed(range(LAYERS)):
        flowing, part_qkv, part_out, part_gain = backward(flowing, norm_gains[layer_index], qkv_weight[layer_index], out_weight[layer_index], saved_layers[layer_index])
        qkv_list[layer_index] = merge_parts(part_qkv)
        out_list[layer_index] = merge_parts(part_out)
        gain_list[layer_index] = merge_parts(part_gain)
    return (jnp.stack(qkv_list), jnp.stack(out_list), jnp.stack(gain_list))
```

```python
import jax
import jax.numpy as jnp
from jax import lax
from jax.sharding import PartitionSpec as P

HD = 128
GROUP = 4
BLOCK = 32


EPSILON = 1e-05
HIGH = lax.Precision.HIGHEST


def from_behind(value, axis, steps):
    count = lax.axis_size(axis)
    leading, last = (max(0, -steps), min(count, count - steps))
    return lax.ppermute(value, axis, [(source, source + steps) for source in range(leading, last)])


def norm_parts(block_rows, gain_row):
    values = block_rows.astype(jnp.float32)
    recip_rms = lax.rsqrt(jnp.mean(values * values, axis=-1, keepdims=True) + EPSILON)
    normed = values * recip_rms
    return (normed, recip_rms, (normed * gain_row).astype(jnp.bfloat16))


def attend(query_rows, key_rows, value_rows, query_pos, key_pos):
    score_scale = query_rows.shape[-1] ** (-0.5)
    scores = (
        jnp.einsum("rgjd,cgd->gjrc", query_rows, key_rows, preferred_element_type=jnp.float32)
        * score_scale
    )
    allowed = key_pos[None, :] <= query_pos[:, None]
    scores = jnp.where(allowed, scores, -jnp.inf)
    row_max = jnp.max(scores, axis=-1, keepdims=True)
    raised = jnp.exp(scores - row_max)
    attn_probs = raised / jnp.sum(raised, axis=-1, keepdims=True)
    probs_low = attn_probs.astype(jnp.bfloat16)
    mixed_rows = jnp.einsum(
        "gjrc,cgd->rgjd", probs_low, value_rows, preferred_element_type=jnp.float32
    )
    return (attn_probs, probs_low, mixed_rows.astype(jnp.bfloat16))


def attend_back(query_rows, key_rows, value_rows, attn_probs, probs_low, grad_mixed):
    score_scale = query_rows.shape[-1] ** (-0.5)
    grad_low = jnp.einsum(
        "rgjd,cgd->gjrc", grad_mixed, value_rows, preferred_element_type=jnp.float32
    )
    inner_sum = jnp.sum(attn_probs * grad_low, axis=-1, keepdims=True)
    grad_score = attn_probs * (grad_low - inner_sum) * score_scale
    grad_query = jnp.einsum(
        "gjrc,cgd->rgjd", grad_score, key_rows.astype(jnp.float32), precision=HIGH
    )
    grad_key = jnp.einsum(
        "gjrc,rgjd->cgd", grad_score, query_rows.astype(jnp.float32), precision=HIGH
    )
    grad_value = jnp.einsum(
        "gjrc,rgjd->cgd", probs_low, grad_mixed, preferred_element_type=jnp.float32
    )
    return (grad_query, grad_key, grad_value)


def heads_total(partial_rows):
    return lax.psum(partial_rows.astype(jnp.bfloat16), "tensor").astype(jnp.float32)


def pass_section(block_value, offset):
    return from_behind(block_value, "pipe", offset)


def keep_active(active, fresh_state, old_state):
    return jax.tree.map(lambda fresh, old: jnp.where(active, fresh, old), fresh_state, old_state)


def shards(tokens, norm_gains, qkv_weight, out_weight, cotangent):
    sections = lax.axis_size("pipe")
    section_index = lax.axis_index("pipe")
    qkv_cols = qkv_weight.shape[2]
    joined = jnp.concatenate([qkv_weight, out_weight], axis=2)
    joined_full = lax.all_gather(joined, "dp", axis=1, tiled=True)[0]
    qkv_local = joined_full[:, :qkv_cols]
    out_local = joined_full[:, qkv_cols:]
    gain_row = norm_gains[0]
    tokens_local = tokens[0]
    grads_local = cotangent[0]
    seq_len = tokens_local.shape[0]
    proj_cols = qkv_local.shape[1]
    groups = proj_cols // ((GROUP + 2) * HD)
    head_cols = groups * GROUP * HD
    positions = jnp.arange(seq_len)
    contract_last = (((1,), (1,)), ((), ()))
    contract_rows = (((0,), (0,)), ((), ()))

    def forward_pass(block_in):
        normed, recip_rms, normed_low = norm_parts(block_in, gain_row)
        projected = jnp.dot(normed_low, qkv_local, preferred_element_type=jnp.float32).reshape(
            seq_len, groups, GROUP + 2, HD
        )
        query_rows = projected[:, :, :GROUP].astype(jnp.bfloat16)
        key_rows = projected[:, :, GROUP].astype(jnp.bfloat16)
        value_rows = projected[:, :, GROUP + 1].astype(jnp.bfloat16)
        attn_probs, probs_low, mixed_rows = attend(
            query_rows, key_rows, value_rows, positions, positions
        )
        flat_mixed = mixed_rows.reshape(seq_len, head_cols)
        partial_rows = lax.dot_general(
            flat_mixed, out_local, contract_last, preferred_element_type=jnp.float32
        )
        summed_heads = heads_total(partial_rows)
        block_out = (block_in.astype(jnp.float32) + summed_heads).astype(jnp.bfloat16)
        saved = (normed, recip_rms, normed_low, query_rows, key_rows, value_rows,
                 attn_probs, probs_low, flat_mixed)
        return block_out, saved

    def backward_pass(grad_in, saved):
        (normed, recip_rms, normed_low, query_rows, key_rows, value_rows,
         attn_probs, probs_low, flat_mixed) = saved
        grad_mixed = (
            jnp.dot(grad_in, out_local, preferred_element_type=jnp.float32)
            .astype(jnp.bfloat16)
            .reshape(seq_len, groups, GROUP, HD)
        )
        grad_query, grad_key, grad_value = attend_back(
            query_rows, key_rows, value_rows, attn_probs, probs_low, grad_mixed
        )
        grad_proj = jnp.concatenate(
            [
                grad_query.astype(jnp.bfloat16),
                grad_key.astype(jnp.bfloat16)[:, :, None],
                grad_value.astype(jnp.bfloat16)[:, :, None],
            ],
            axis=2,
        ).reshape(seq_len, proj_cols)
        partial_rows = lax.dot_general(
            grad_proj, qkv_local, contract_last, preferred_element_type=jnp.float32
        )
        grad_normed = heads_total(partial_rows).astype(jnp.bfloat16)
        grad_float = grad_normed.astype(jnp.float32)
        scaled = grad_float * gain_row
        grad_norm_in = recip_rms * (
            scaled - normed * jnp.mean(scaled * normed, axis=-1, keepdims=True)
        )
        block_out = (grad_in.astype(jnp.float32) + grad_norm_in).astype(jnp.bfloat16)
        gain_part = jnp.sum(grad_float * normed, axis=0)
        return block_out, (grad_proj, gain_part)

    incoming = jnp.zeros_like(tokens_local)
    for turn in range(sections):
        block_in = jnp.where(section_index == 0, tokens_local, incoming)
        block_out, saved = forward_pass(block_in)
        if turn < sections - 1:
            incoming = pass_section(block_out, 1)

    incoming = jnp.zeros_like(grads_local)
    for turn in range(sections):
        grad_in = jnp.where(section_index == sections - 1, grads_local, incoming)
        grad_out, (grad_proj, gain_part) = backward_pass(grad_in, saved)
        if turn < sections - 1:
            incoming = pass_section(grad_out, -1)

    normed_low = saved[2]
    flat_mixed = saved[8]
    weight_part = lax.dot_general(
        normed_low, grad_proj, contract_rows, preferred_element_type=jnp.float32
    )
    output_part = lax.dot_general(
        grad_in, flat_mixed, contract_rows, preferred_element_type=jnp.float32
    )
    parts = jnp.concatenate(
        [
            weight_part.astype(jnp.bfloat16),
            output_part.astype(jnp.bfloat16),
            gain_part[:, None].astype(jnp.bfloat16),
        ],
        axis=1,
    )
    reduced = lax.psum_scatter(parts, "dp", scatter_dimension=0, tiled=True).astype(jnp.float32)
    qkv_result = reduced[None, :, :proj_cols]
    out_result = reduced[None, :, proj_cols : proj_cols + head_cols]
    gain_result = reduced[None, :, proj_cols + head_cols]
    return (qkv_result, out_result, gain_result)


def solution(mesh):
    in_specs = (
        P("dp", None, None),
        P("pipe", None),
        P("pipe", "dp", "tensor"),
        P("pipe", "dp", "tensor"),
        P("dp", None, None),
    )
    out_specs = (P("pipe", "dp", "tensor"), P("pipe", "dp", "tensor"), P("pipe", "dp"))
    return jax.shard_map(shards, mesh=mesh, in_specs=in_specs, out_specs=out_specs, check_vma=False)
```

```python
import jax
import jax.numpy as jnp
from jax import lax
from jax.sharding import PartitionSpec as P

HD = 128
GROUP = 4
BLOCK = 32


EPSILON = 1e-05
HIGH = lax.Precision.HIGHEST


def from_behind(value, axis, steps):
    count = lax.axis_size(axis)
    leading, last = (max(0, -steps), min(count, count - steps))
    return lax.ppermute(value, axis, [(source, source + steps) for source in range(leading, last)])


def norm_parts(block_rows, gain_row):
    values = block_rows.astype(jnp.float32)
    recip_rms = lax.rsqrt(jnp.mean(values * values, axis=-1, keepdims=True) + EPSILON)
    normed = values * recip_rms
    return (normed, recip_rms, (normed * gain_row).astype(jnp.bfloat16))


def attend(query_rows, key_rows, value_rows, query_pos, key_pos):
    score_scale = query_rows.shape[-1] ** (-0.5)
    scores = (
        jnp.einsum("rgjd,cgd->gjrc", query_rows, key_rows, preferred_element_type=jnp.float32)
        * score_scale
    )
    allowed = key_pos[None, :] <= query_pos[:, None]
    scores = jnp.where(allowed, scores, -jnp.inf)
    row_max = jnp.max(scores, axis=-1, keepdims=True)
    raised = jnp.exp(scores - row_max)
    attn_probs = raised / jnp.sum(raised, axis=-1, keepdims=True)
    probs_low = attn_probs.astype(jnp.bfloat16)
    mixed_rows = jnp.einsum(
        "gjrc,cgd->rgjd", probs_low, value_rows, preferred_element_type=jnp.float32
    )
    return (attn_probs, probs_low, mixed_rows.astype(jnp.bfloat16))


def attend_back(query_rows, key_rows, value_rows, attn_probs, probs_low, grad_mixed):
    score_scale = query_rows.shape[-1] ** (-0.5)
    grad_low = jnp.einsum(
        "rgjd,cgd->gjrc", grad_mixed, value_rows, preferred_element_type=jnp.float32
    )
    inner_sum = jnp.sum(attn_probs * grad_low, axis=-1, keepdims=True)
    grad_score = attn_probs * (grad_low - inner_sum) * score_scale
    grad_query = jnp.einsum(
        "gjrc,cgd->rgjd", grad_score, key_rows.astype(jnp.float32), precision=HIGH
    )
    grad_key = jnp.einsum(
        "gjrc,rgjd->cgd", grad_score, query_rows.astype(jnp.float32), precision=HIGH
    )
    grad_value = jnp.einsum(
        "gjrc,rgjd->cgd", probs_low, grad_mixed, preferred_element_type=jnp.float32
    )
    return (grad_query, grad_key, grad_value)


def exchange(value, axis, mask):
    count = lax.axis_size(axis)
    return lax.ppermute(value, axis, [(source, source ^ mask) for source in range(count)])


def heads_total(partial_rows):
    count = lax.axis_size("tensor")
    low_bit = lax.axis_index("tensor") % 2
    rows = partial_rows.shape[0]
    half = rows // 2
    values = partial_rows.astype(jnp.bfloat16)
    keep = lax.dynamic_slice_in_dim(values, low_bit * half, half, 0)
    give = lax.dynamic_slice_in_dim(values, (1 - low_bit) * half, half, 0)
    summed = (keep.astype(jnp.float32) + exchange(give, "tensor", 1).astype(jnp.float32)).astype(
        jnp.bfloat16
    )
    mask = 2
    while mask < count:
        summed = (
            summed.astype(jnp.float32) + exchange(summed, "tensor", mask).astype(jnp.float32)
        ).astype(jnp.bfloat16)
        mask *= 2
    other = exchange(summed, "tensor", 1)
    whole = jnp.where(
        low_bit == 0,
        jnp.concatenate([summed, other], axis=0),
        jnp.concatenate([other, summed], axis=0),
    )
    return whole.astype(jnp.float32)


def pass_section(block_value, offset):
    return from_behind(block_value, "pipe", offset)


def keep_active(active, fresh_state, old_state):
    return jax.tree.map(lambda fresh, old: jnp.where(active, fresh, old), fresh_state, old_state)


def shards(tokens, norm_gains, qkv_weight, out_weight, cotangent):
    sections = lax.axis_size("pipe")
    section_index = lax.axis_index("pipe")
    qkv_cols = qkv_weight.shape[2]
    joined = jnp.concatenate([qkv_weight, out_weight], axis=2)
    joined_full = lax.all_gather(joined, "dp", axis=1, tiled=True)[0]
    qkv_local = joined_full[:, :qkv_cols]
    out_local = joined_full[:, qkv_cols:]
    gain_row = norm_gains[0]
    tokens_local = tokens[0]
    grads_local = cotangent[0]
    seq_len = tokens_local.shape[0]
    proj_cols = qkv_local.shape[1]
    groups = proj_cols // ((GROUP + 2) * HD)
    head_cols = groups * GROUP * HD
    positions = jnp.arange(seq_len)
    contract_last = (((1,), (1,)), ((), ()))
    contract_rows = (((0,), (0,)), ((), ()))

    def forward_pass(block_in):
        normed, recip_rms, normed_low = norm_parts(block_in, gain_row)
        projected = lax.optimization_barrier(
            jnp.dot(normed_low, qkv_local, preferred_element_type=jnp.float32)
        ).reshape(seq_len, groups, GROUP + 2, HD)
        query_rows = projected[:, :, :GROUP].astype(jnp.bfloat16)
        key_rows = projected[:, :, GROUP].astype(jnp.bfloat16)
        value_rows = projected[:, :, GROUP + 1].astype(jnp.bfloat16)
        attn_probs, probs_low, mixed_rows = attend(
            query_rows, key_rows, value_rows, positions, positions
        )
        flat_mixed = mixed_rows.reshape(seq_len, head_cols)
        partial_rows = lax.dot_general(
            flat_mixed, out_local, contract_last, preferred_element_type=jnp.float32
        )
        summed_heads = heads_total(partial_rows)
        block_out = (block_in.astype(jnp.float32) + summed_heads).astype(jnp.bfloat16)
        saved = (normed, recip_rms, normed_low, query_rows, key_rows, value_rows,
                 attn_probs, probs_low, flat_mixed)
        return block_out, saved

    def backward_pass(grad_in, saved):
        (normed, recip_rms, normed_low, query_rows, key_rows, value_rows,
         attn_probs, probs_low, flat_mixed) = saved
        grad_mixed = (
            jnp.dot(grad_in, out_local, preferred_element_type=jnp.float32)
            .astype(jnp.bfloat16)
            .reshape(seq_len, groups, GROUP, HD)
        )
        grad_query, grad_key, grad_value = attend_back(
            query_rows, key_rows, value_rows, attn_probs, probs_low, grad_mixed
        )
        grad_proj = jnp.concatenate(
            [
                grad_query.astype(jnp.bfloat16),
                grad_key.astype(jnp.bfloat16)[:, :, None],
                grad_value.astype(jnp.bfloat16)[:, :, None],
            ],
            axis=2,
        ).reshape(seq_len, proj_cols)
        partial_rows = lax.dot_general(
            qkv_local, grad_proj, contract_last, preferred_element_type=jnp.float32
        ).T
        grad_normed = heads_total(partial_rows).astype(jnp.bfloat16)
        grad_float = grad_normed.astype(jnp.float32)
        scaled = grad_float * gain_row
        grad_norm_in = recip_rms * (
            scaled - normed * jnp.mean(scaled * normed, axis=-1, keepdims=True)
        )
        block_out = (grad_in.astype(jnp.float32) + grad_norm_in).astype(jnp.bfloat16)
        gain_part = jnp.sum(grad_float * normed, axis=0)
        return block_out, (grad_proj, gain_part)

    incoming = jnp.zeros_like(tokens_local)
    for turn in range(sections):
        block_in = jnp.where(section_index == 0, tokens_local, incoming)
        block_out, saved = forward_pass(block_in)
        if turn < sections - 1:
            incoming = pass_section(block_out, 1)

    incoming = jnp.zeros_like(grads_local)
    for turn in range(sections):
        grad_in = jnp.where(section_index == sections - 1, grads_local, incoming)
        grad_out, (grad_proj, gain_part) = backward_pass(grad_in, saved)
        if turn < sections - 1:
            incoming = pass_section(grad_out, -1)

    normed_low = saved[2]
    flat_mixed = saved[8]
    weight_part = lax.dot_general(
        normed_low, grad_proj, contract_rows, preferred_element_type=jnp.float32
    )
    output_part = lax.dot_general(
        grad_in, flat_mixed, contract_rows, preferred_element_type=jnp.float32
    )
    parts = jnp.concatenate(
        [
            weight_part.astype(jnp.bfloat16),
            output_part.astype(jnp.bfloat16),
            gain_part[:, None].astype(jnp.bfloat16),
        ],
        axis=1,
    )
    reduced = lax.psum_scatter(parts, "dp", scatter_dimension=0, tiled=True).astype(jnp.float32)
    qkv_result = reduced[None, :, :proj_cols]
    out_result = reduced[None, :, proj_cols : proj_cols + head_cols]
    gain_result = reduced[None, :, proj_cols + head_cols]
    return (qkv_result, out_result, gain_result)


def solution(mesh):
    in_specs = (
        P("dp", None, None),
        P("pipe", None),
        P("pipe", "dp", "tensor"),
        P("pipe", "dp", "tensor"),
        P("dp", None, None),
    )
    out_specs = (P("pipe", "dp", "tensor"), P("pipe", "dp", "tensor"), P("pipe", "dp"))
    return jax.shard_map(shards, mesh=mesh, in_specs=in_specs, out_specs=out_specs, check_vma=False)
```

```python
import jax
import jax.numpy as jnp
from jax import lax
from jax.sharding import PartitionSpec as P

HD = 128
GROUP = 4
BLOCK = 32


EPSILON = 1e-05
HIGH = lax.Precision.HIGHEST


def from_behind(value, axis, steps):
    count = lax.axis_size(axis)
    leading, last = (max(0, -steps), min(count, count - steps))
    return lax.ppermute(value, axis, [(source, source + steps) for source in range(leading, last)])


def norm_parts(block_rows, gain_row):
    values = block_rows.astype(jnp.float32)
    recip_rms = lax.rsqrt(jnp.mean(values * values, axis=-1, keepdims=True) + EPSILON)
    normed = values * recip_rms
    return (normed, recip_rms, (normed * gain_row).astype(jnp.bfloat16))


def attend(query_rows, key_rows, value_rows, query_pos, key_pos):
    score_scale = query_rows.shape[-1] ** (-0.5)
    scores = (
        jnp.einsum("rgjd,cgd->gjrc", query_rows, key_rows, preferred_element_type=jnp.float32)
        * score_scale
    )
    allowed = key_pos[None, :] <= query_pos[:, None]
    scores = jnp.where(allowed, scores, -jnp.inf)
    row_max = jnp.max(scores, axis=-1, keepdims=True)
    raised = jnp.exp(scores - row_max)
    attn_probs = raised / jnp.sum(raised, axis=-1, keepdims=True)
    probs_low = attn_probs.astype(jnp.bfloat16)
    mixed_rows = jnp.einsum(
        "gjrc,cgd->rgjd", probs_low, value_rows, preferred_element_type=jnp.float32
    )
    return (attn_probs, probs_low, mixed_rows.astype(jnp.bfloat16))


def attend_back(query_rows, key_rows, value_rows, attn_probs, probs_low, grad_mixed):
    score_scale = query_rows.shape[-1] ** (-0.5)
    grad_low = jnp.einsum(
        "rgjd,cgd->gjrc", grad_mixed, value_rows, preferred_element_type=jnp.float32
    )
    inner_sum = jnp.sum(attn_probs * grad_low, axis=-1, keepdims=True)
    grad_score = attn_probs * (grad_low - inner_sum) * score_scale
    grad_query = jnp.einsum(
        "gjrc,cgd->rgjd", grad_score, key_rows.astype(jnp.float32), precision=HIGH
    )
    grad_key = jnp.einsum(
        "gjrc,rgjd->cgd", grad_score, query_rows.astype(jnp.float32), precision=HIGH
    )
    grad_value = jnp.einsum(
        "gjrc,rgjd->cgd", probs_low, grad_mixed, preferred_element_type=jnp.float32
    )
    return (grad_query, grad_key, grad_value)


def exchange(value, axis, mask):
    count = lax.axis_size(axis)
    return lax.ppermute(value, axis, [(source, source ^ mask) for source in range(count)])


def tensor_scatter(partial_rows):
    count = lax.axis_size("tensor")
    member = lax.axis_index("tensor")
    values = partial_rows.astype(jnp.bfloat16)
    offset = 0
    mask = 1
    while mask < count:
        bit = (member // mask) % 2
        half = values.shape[0] // 2
        keep = lax.dynamic_slice_in_dim(values, bit * half, half, 0)
        give = lax.dynamic_slice_in_dim(values, (1 - bit) * half, half, 0)
        values = (
            keep.astype(jnp.float32) + exchange(give, "tensor", mask).astype(jnp.float32)
        ).astype(jnp.bfloat16)
        offset = offset + bit * half
        mask *= 2
    return values, offset


def tensor_gather(block):
    count = lax.axis_size("tensor")
    member = lax.axis_index("tensor")
    values = block
    mask = count // 2
    while mask >= 1:
        bit = (member // mask) % 2
        other = exchange(values, "tensor", mask)
        values = jnp.where(
            bit == 0,
            jnp.concatenate([values, other], axis=0),
            jnp.concatenate([other, values], axis=0),
        )
        mask //= 2
    return values


def tensor_total(vector):
    count = lax.axis_size("tensor")
    mask = 1
    while mask < count:
        vector = vector + exchange(vector, "tensor", mask)
        mask *= 2
    return vector


def pass_section(block_value, offset):
    return from_behind(block_value, "pipe", offset)


def keep_active(active, fresh_state, old_state):
    return jax.tree.map(lambda fresh, old: jnp.where(active, fresh, old), fresh_state, old_state)


def shards(tokens, norm_gains, qkv_weight, out_weight, cotangent):
    sections = lax.axis_size("pipe")
    section_index = lax.axis_index("pipe")
    qkv_cols = qkv_weight.shape[2]
    joined = jnp.concatenate([qkv_weight, out_weight], axis=2)
    joined_full = lax.all_gather(joined, "dp", axis=1, tiled=True)[0]
    qkv_local = joined_full[:, :qkv_cols]
    out_local = joined_full[:, qkv_cols:]
    gain_row = norm_gains[0]
    tokens_local = tokens[0]
    grads_local = cotangent[0]
    seq_len = tokens_local.shape[0]
    model_width = tokens_local.shape[1]
    proj_cols = qkv_local.shape[1]
    groups = proj_cols // ((GROUP + 2) * HD)
    head_cols = groups * GROUP * HD
    positions = jnp.arange(seq_len)
    contract_last = (((1,), (1,)), ((), ()))
    contract_rows = (((0,), (0,)), ((), ()))

    def forward_pass(block_in):
        normed, recip_rms, normed_low = norm_parts(block_in, gain_row)
        projected = lax.optimization_barrier(
            jnp.dot(normed_low, qkv_local, preferred_element_type=jnp.float32)
        ).reshape(seq_len, groups, GROUP + 2, HD)
        query_rows = projected[:, :, :GROUP].astype(jnp.bfloat16)
        key_rows = projected[:, :, GROUP].astype(jnp.bfloat16)
        value_rows = projected[:, :, GROUP + 1].astype(jnp.bfloat16)
        attn_probs, probs_low, mixed_rows = attend(
            query_rows, key_rows, value_rows, positions, positions
        )
        flat_mixed = mixed_rows.reshape(seq_len, head_cols)
        partial_rows = lax.dot_general(
            flat_mixed, out_local, contract_last, preferred_element_type=jnp.float32
        )
        summed_rows, offset = tensor_scatter(partial_rows)
        rows_in = lax.dynamic_slice_in_dim(block_in, offset, summed_rows.shape[0], 0)
        rows_out = (rows_in.astype(jnp.float32) + summed_rows.astype(jnp.float32)).astype(
            jnp.bfloat16
        )
        saved = (normed, recip_rms, normed_low, query_rows, key_rows, value_rows,
                 attn_probs, probs_low, flat_mixed)
        return rows_out, saved

    def backward_pass(grad_in, saved):
        (normed, recip_rms, normed_low, query_rows, key_rows, value_rows,
         attn_probs, probs_low, flat_mixed) = saved
        grad_mixed = (
            jnp.dot(grad_in, out_local, preferred_element_type=jnp.float32)
            .astype(jnp.bfloat16)
            .reshape(seq_len, groups, GROUP, HD)
        )
        grad_query, grad_key, grad_value = attend_back(
            query_rows, key_rows, value_rows, attn_probs, probs_low, grad_mixed
        )
        grad_proj = jnp.concatenate(
            [
                grad_query.astype(jnp.bfloat16),
                grad_key.astype(jnp.bfloat16)[:, :, None],
                grad_value.astype(jnp.bfloat16)[:, :, None],
            ],
            axis=2,
        ).reshape(seq_len, proj_cols)
        partial_rows = lax.dot_general(
            qkv_local, grad_proj, contract_last, preferred_element_type=jnp.float32
        ).T
        grad_rows, offset = tensor_scatter(partial_rows)
        count = grad_rows.shape[0]
        normed_rows = lax.dynamic_slice_in_dim(normed, offset, count, 0)
        recip_rows = lax.dynamic_slice_in_dim(recip_rms, offset, count, 0)
        grad_in_rows = lax.dynamic_slice_in_dim(grad_in, offset, count, 0)
        grad_float = grad_rows.astype(jnp.float32)
        scaled = grad_float * gain_row
        grad_norm_in = recip_rows * (
            scaled - normed_rows * jnp.mean(scaled * normed_rows, axis=-1, keepdims=True)
        )
        rows_out = (grad_in_rows.astype(jnp.float32) + grad_norm_in).astype(jnp.bfloat16)
        gain_part = jnp.sum(grad_float * normed_rows, axis=0)
        return rows_out, (grad_proj, gain_part)

    incoming = jnp.zeros_like(tokens_local)
    for turn in range(sections):
        block_in = jnp.where(section_index == 0, tokens_local, incoming)
        rows_out, saved = forward_pass(block_in)
        if turn < sections - 1:
            incoming = tensor_gather(pass_section(rows_out, 1))

    incoming = jnp.zeros_like(grads_local)
    for turn in range(sections):
        grad_in = jnp.where(section_index == sections - 1, grads_local, incoming)
        rows_out, (grad_proj, gain_part) = backward_pass(grad_in, saved)
        if turn < sections - 1:
            incoming = tensor_gather(pass_section(rows_out, -1))

    normed_low = saved[2]
    flat_mixed = saved[8]
    gain_total = tensor_total(gain_part)
    pad_rows = 8
    gain_cols = 128
    left = jnp.concatenate(
        [
            normed_low,
            grad_in,
            jnp.zeros((pad_rows, model_width), jnp.bfloat16).at[0].set(gain_total.astype(jnp.bfloat16)),
        ],
        axis=0,
    )
    right = jnp.concatenate(
        [
            jnp.pad(grad_proj, ((0, 0), (0, head_cols + gain_cols))),
            jnp.pad(flat_mixed, ((0, 0), (proj_cols, gain_cols))),
            jnp.zeros((pad_rows, proj_cols + head_cols + gain_cols), jnp.bfloat16)
            .at[0, proj_cols + head_cols]
            .set(1.0),
        ],
        axis=0,
    )
    parts = lax.dot_general(
        left, right, contract_rows, preferred_element_type=jnp.float32
    ).astype(jnp.bfloat16)
    reduced = lax.psum_scatter(parts, "dp", scatter_dimension=0, tiled=True).astype(jnp.float32)
    qkv_result = reduced[None, :, :proj_cols]
    out_result = reduced[None, :, proj_cols : proj_cols + head_cols]
    gain_result = reduced[None, :, proj_cols + head_cols]
    return (qkv_result, out_result, gain_result)


def solution(mesh):
    in_specs = (
        P("dp", None, None),
        P("pipe", None),
        P("pipe", "dp", "tensor"),
        P("pipe", "dp", "tensor"),
        P("dp", None, None),
    )
    out_specs = (P("pipe", "dp", "tensor"), P("pipe", "dp", "tensor"), P("pipe", "dp"))
    return jax.shard_map(shards, mesh=mesh, in_specs=in_specs, out_specs=out_specs, check_vma=False)
```

```python
import jax
import jax.numpy as jnp
from jax import lax
from jax.sharding import PartitionSpec as P

HD = 128
GROUP = 4
BLOCK = 32


EPSILON = 1e-05
HIGH = lax.Precision.HIGHEST


def from_behind(value, axis, steps):
    count = lax.axis_size(axis)
    leading, last = (max(0, -steps), min(count, count - steps))
    return lax.ppermute(value, axis, [(source, source + steps) for source in range(leading, last)])


def norm_parts(block_rows, gain_row):
    values = block_rows.astype(jnp.float32)
    recip_rms = lax.rsqrt(jnp.mean(values * values, axis=-1, keepdims=True) + EPSILON)
    normed = values * recip_rms
    return (normed, recip_rms, (normed * gain_row).astype(jnp.bfloat16))


def attend(query_rows, key_rows, value_rows, query_pos, key_pos):
    score_scale = query_rows.shape[-1] ** (-0.5)
    scores = (
        jnp.einsum("rgjd,cgd->gjrc", query_rows, key_rows, preferred_element_type=jnp.float32)
        * score_scale
    )
    allowed = key_pos[None, :] <= query_pos[:, None]
    scores = jnp.where(allowed, scores, -jnp.inf)
    row_max = jnp.max(scores, axis=-1, keepdims=True)
    raised = jnp.exp(scores - row_max)
    attn_probs = raised / jnp.sum(raised, axis=-1, keepdims=True)
    probs_low = attn_probs.astype(jnp.bfloat16)
    mixed_rows = jnp.einsum(
        "gjrc,cgd->rgjd", probs_low, value_rows, preferred_element_type=jnp.float32
    )
    return (attn_probs, probs_low, mixed_rows.astype(jnp.bfloat16))


def attend_back(query_rows, key_rows, value_rows, attn_probs, probs_low, grad_mixed):
    score_scale = query_rows.shape[-1] ** (-0.5)
    grad_low = jnp.einsum(
        "rgjd,cgd->gjrc", grad_mixed, value_rows, preferred_element_type=jnp.float32
    )
    inner_sum = jnp.sum(attn_probs * grad_low, axis=-1, keepdims=True)
    grad_score = attn_probs * (grad_low - inner_sum) * score_scale
    grad_query = jnp.einsum(
        "gjrc,cgd->rgjd", grad_score, key_rows.astype(jnp.float32), precision=HIGH
    )
    grad_key = jnp.einsum(
        "gjrc,rgjd->cgd", grad_score, query_rows.astype(jnp.float32), precision=HIGH
    )
    grad_value = jnp.einsum(
        "gjrc,rgjd->cgd", probs_low, grad_mixed, preferred_element_type=jnp.float32
    )
    return (grad_query, grad_key, grad_value)


def exchange(value, axis, mask):
    count = lax.axis_size(axis)
    return lax.ppermute(value, axis, [(source, source ^ mask) for source in range(count)])


def tensor_scatter(partial_rows):
    count = lax.axis_size("tensor")
    member = lax.axis_index("tensor")
    values = partial_rows.astype(jnp.bfloat16)
    offset = 0
    mask = 1
    while mask < count:
        bit = (member // mask) % 2
        half = values.shape[0] // 2
        keep = lax.dynamic_slice_in_dim(values, bit * half, half, 0)
        give = lax.dynamic_slice_in_dim(values, (1 - bit) * half, half, 0)
        values = (
            keep.astype(jnp.float32) + exchange(give, "tensor", mask).astype(jnp.float32)
        ).astype(jnp.bfloat16)
        offset = offset + bit * half
        mask *= 2
    return values, offset


def tensor_gather(block):
    count = lax.axis_size("tensor")
    member = lax.axis_index("tensor")
    values = block
    mask = count // 2
    while mask >= 1:
        bit = (member // mask) % 2
        other = exchange(values, "tensor", mask)
        values = jnp.where(
            bit == 0,
            jnp.concatenate([values, other], axis=0),
            jnp.concatenate([other, values], axis=0),
        )
        mask //= 2
    return values


def tensor_total(vector):
    count = lax.axis_size("tensor")
    mask = 1
    while mask < count:
        vector = vector + exchange(vector, "tensor", mask)
        mask *= 2
    return vector


def dp_total(vector):
    count = lax.axis_size("dp")
    mask = 1
    while mask < count:
        vector = vector + exchange(vector, "dp", mask)
        mask *= 2
    return vector


def pass_section(block_value, offset):
    return from_behind(block_value, "pipe", offset)


def keep_active(active, fresh_state, old_state):
    return jax.tree.map(lambda fresh, old: jnp.where(active, fresh, old), fresh_state, old_state)


def shards(tokens, norm_gains, qkv_weight, out_weight, cotangent):
    sections = lax.axis_size("pipe")
    section_index = lax.axis_index("pipe")
    qkv_cols = qkv_weight.shape[2]
    joined = jnp.concatenate([qkv_weight, out_weight], axis=2)
    joined_full = lax.all_gather(joined, "dp", axis=1, tiled=True)[0]
    qkv_local = joined_full[:, :qkv_cols]
    out_local = joined_full[:, qkv_cols:]
    gain_row = norm_gains[0]
    tokens_local = tokens[0]
    grads_local = cotangent[0]
    seq_len = tokens_local.shape[0]
    model_width = tokens_local.shape[1]
    proj_cols = qkv_local.shape[1]
    groups = proj_cols // ((GROUP + 2) * HD)
    head_cols = groups * GROUP * HD
    positions = jnp.arange(seq_len)
    contract_last = (((1,), (1,)), ((), ()))
    contract_rows = (((0,), (0,)), ((), ()))

    def forward_pass(block_in):
        normed, recip_rms, normed_low = norm_parts(block_in, gain_row)
        projected = lax.optimization_barrier(
            jnp.dot(normed_low, qkv_local, preferred_element_type=jnp.float32)
        ).reshape(seq_len, groups, GROUP + 2, HD)
        query_rows = projected[:, :, :GROUP].astype(jnp.bfloat16)
        key_rows = projected[:, :, GROUP].astype(jnp.bfloat16)
        value_rows = projected[:, :, GROUP + 1].astype(jnp.bfloat16)
        attn_probs, probs_low, mixed_rows = attend(
            query_rows, key_rows, value_rows, positions, positions
        )
        flat_mixed = mixed_rows.reshape(seq_len, head_cols)
        partial_rows = lax.dot_general(
            flat_mixed, out_local, contract_last, preferred_element_type=jnp.float32
        )
        summed_rows, offset = tensor_scatter(partial_rows)
        rows_in = lax.dynamic_slice_in_dim(block_in, offset, summed_rows.shape[0], 0)
        rows_out = (rows_in.astype(jnp.float32) + summed_rows.astype(jnp.float32)).astype(
            jnp.bfloat16
        )
        saved = (normed, recip_rms, normed_low, query_rows, key_rows, value_rows,
                 attn_probs, probs_low, flat_mixed)
        return rows_out, saved

    def backward_pass(grad_in, saved):
        (normed, recip_rms, normed_low, query_rows, key_rows, value_rows,
         attn_probs, probs_low, flat_mixed) = saved
        grad_mixed = (
            jnp.dot(grad_in, out_local, preferred_element_type=jnp.float32)
            .astype(jnp.bfloat16)
            .reshape(seq_len, groups, GROUP, HD)
        )
        grad_query, grad_key, grad_value = attend_back(
            query_rows, key_rows, value_rows, attn_probs, probs_low, grad_mixed
        )
        grad_proj = jnp.concatenate(
            [
                grad_query.astype(jnp.bfloat16),
                grad_key.astype(jnp.bfloat16)[:, :, None],
                grad_value.astype(jnp.bfloat16)[:, :, None],
            ],
            axis=2,
        ).reshape(seq_len, proj_cols)
        partial_rows = lax.dot_general(
            qkv_local, grad_proj, contract_last, preferred_element_type=jnp.float32
        ).T
        grad_rows, offset = tensor_scatter(partial_rows)
        count = grad_rows.shape[0]
        normed_rows = lax.dynamic_slice_in_dim(normed, offset, count, 0)
        recip_rows = lax.dynamic_slice_in_dim(recip_rms, offset, count, 0)
        grad_in_rows = lax.dynamic_slice_in_dim(grad_in, offset, count, 0)
        grad_float = grad_rows.astype(jnp.float32)
        scaled = grad_float * gain_row
        grad_norm_in = recip_rows * (
            scaled - normed_rows * jnp.mean(scaled * normed_rows, axis=-1, keepdims=True)
        )
        rows_out = (grad_in_rows.astype(jnp.float32) + grad_norm_in).astype(jnp.bfloat16)
        gain_part = jnp.sum(grad_float * normed_rows, axis=0)
        return rows_out, (grad_proj, gain_part)

    incoming = jnp.zeros_like(tokens_local)
    for turn in range(sections):
        block_in = jnp.where(section_index == 0, tokens_local, incoming)
        rows_out, saved = forward_pass(block_in)
        if turn < sections - 1:
            incoming = tensor_gather(pass_section(rows_out, 1))

    incoming = jnp.zeros_like(grads_local)
    for turn in range(sections):
        grad_in = jnp.where(section_index == sections - 1, grads_local, incoming)
        rows_out, (grad_proj, gain_part) = backward_pass(grad_in, saved)
        if turn < sections - 1:
            incoming = tensor_gather(pass_section(rows_out, -1))

    normed_low = saved[2]
    flat_mixed = saved[8]
    seqs = lax.axis_size("dp")
    slice_width = model_width // seqs
    normed_cols = lax.all_to_all(normed_low, "dp", 1, 0, tiled=True)
    mixed_rows = lax.all_gather(flat_mixed, "dp", axis=0, tiled=True)
    grad_cols = lax.all_to_all(grad_in, "dp", 1, 0, tiled=True)
    dproj_rows = lax.all_gather(grad_proj, "dp", axis=0, tiled=True)
    qkv_result = lax.dot_general(
        normed_cols, dproj_rows, contract_rows, preferred_element_type=jnp.float32
    )[None]
    out_result = lax.dot_general(
        grad_cols, mixed_rows, contract_rows, preferred_element_type=jnp.float32
    )[None]
    gain_total = dp_total(tensor_total(gain_part))
    gain_result = lax.dynamic_slice_in_dim(
        gain_total, lax.axis_index("dp") * slice_width, slice_width, 0
    )[None]
    return (qkv_result, out_result, gain_result)


def solution(mesh):
    in_specs = (
        P("dp", None, None),
        P("pipe", None),
        P("pipe", "dp", "tensor"),
        P("pipe", "dp", "tensor"),
        P("dp", None, None),
    )
    out_specs = (P("pipe", "dp", "tensor"), P("pipe", "dp", "tensor"), P("pipe", "dp"))
    return jax.shard_map(shards, mesh=mesh, in_specs=in_specs, out_specs=out_specs, check_vma=False)
```

```python
import jax
import jax.numpy as jnp
from jax import lax
from jax.sharding import PartitionSpec as P

HD = 128
GROUP = 4
BLOCK = 32


EPSILON = 1e-05
HIGH = lax.Precision.HIGHEST


def from_behind(value, axis, steps):
    count = lax.axis_size(axis)
    leading, last = (max(0, -steps), min(count, count - steps))
    return lax.ppermute(value, axis, [(source, source + steps) for source in range(leading, last)])


def norm_parts(block_rows, gain_row):
    values = block_rows.astype(jnp.float32)
    recip_rms = lax.rsqrt(jnp.mean(values * values, axis=-1, keepdims=True) + EPSILON)
    normed = values * recip_rms
    return (normed, recip_rms, (normed * gain_row).astype(jnp.bfloat16))


def attend(query_rows, key_rows, value_rows, query_pos, key_pos):
    score_scale = query_rows.shape[-1] ** (-0.5)
    scores = (
        jnp.einsum("rgjd,cgd->gjrc", query_rows, key_rows, preferred_element_type=jnp.float32)
        * score_scale
    )
    allowed = key_pos[None, :] <= query_pos[:, None]
    scores = jnp.where(allowed, scores, -jnp.inf)
    row_max = jnp.max(scores, axis=-1, keepdims=True)
    raised = jnp.exp(scores - row_max)
    attn_probs = raised / jnp.sum(raised, axis=-1, keepdims=True)
    probs_low = attn_probs.astype(jnp.bfloat16)
    mixed_rows = jnp.einsum(
        "gjrc,cgd->rgjd", probs_low, value_rows, preferred_element_type=jnp.float32
    )
    return (attn_probs, probs_low, mixed_rows.astype(jnp.bfloat16))


def attend_back(query_rows, key_rows, value_rows, attn_probs, probs_low, grad_mixed):
    score_scale = query_rows.shape[-1] ** (-0.5)
    grad_low = jnp.einsum(
        "rgjd,cgd->gjrc", grad_mixed, value_rows, preferred_element_type=jnp.float32
    )
    inner_sum = jnp.sum(attn_probs * grad_low, axis=-1, keepdims=True)
    grad_score = attn_probs * (grad_low - inner_sum) * score_scale
    grad_query = jnp.einsum(
        "gjrc,cgd->rgjd", grad_score, key_rows.astype(jnp.float32), precision=HIGH
    )
    grad_key = jnp.einsum(
        "gjrc,rgjd->cgd", grad_score, query_rows.astype(jnp.float32), precision=HIGH
    )
    grad_value = jnp.einsum(
        "gjrc,rgjd->cgd", probs_low, grad_mixed, preferred_element_type=jnp.float32
    )
    return (grad_query, grad_key, grad_value)


def exchange(value, axis, mask):
    count = lax.axis_size(axis)
    return lax.ppermute(value, axis, [(source, source ^ mask) for source in range(count)])


def tensor_scatter(partial_rows):
    count = lax.axis_size("tensor")
    member = lax.axis_index("tensor")
    values = partial_rows.astype(jnp.bfloat16)
    offset = 0
    mask = 1
    while mask < count:
        bit = (member // mask) % 2
        half = values.shape[0] // 2
        keep = lax.dynamic_slice_in_dim(values, bit * half, half, 0)
        give = lax.dynamic_slice_in_dim(values, (1 - bit) * half, half, 0)
        values = (
            keep.astype(jnp.float32) + exchange(give, "tensor", mask).astype(jnp.float32)
        ).astype(jnp.bfloat16)
        offset = offset + bit * half
        mask *= 2
    return values, offset


def tensor_gather(block):
    count = lax.axis_size("tensor")
    member = lax.axis_index("tensor")
    values = block
    mask = count // 2
    while mask >= 1:
        bit = (member // mask) % 2
        other = exchange(values, "tensor", mask)
        values = jnp.where(
            bit == 0,
            jnp.concatenate([values, other], axis=0),
            jnp.concatenate([other, values], axis=0),
        )
        mask //= 2
    return values


def tensor_total(vector):
    count = lax.axis_size("tensor")
    mask = 1
    while mask < count:
        vector = vector + exchange(vector, "tensor", mask)
        mask *= 2
    return vector


def group_total(vector, axis, stride, size):
    count = lax.axis_size(axis)
    member = lax.axis_index(axis)
    digit = (member // stride) % size

    def moved(source, shift):
        source_digit = (source // stride) % size
        return source + ((source_digit + shift) % size - source_digit) * stride

    received = [vector] + [
        lax.ppermute(vector, axis, [(source, moved(source, shift)) for source in range(count)])
        for shift in range(1, size)
    ]
    stacked = jnp.stack(received)
    ordered = [stacked[(digit - j) % size] for j in range(size)]
    while len(ordered) > 1:
        ordered = [ordered[i] + ordered[i + 1] for i in range(0, len(ordered), 2)]
    return ordered[0]


def axis_total(vector, axis):
    count = lax.axis_size(axis)
    stride = 1
    while stride < count:
        size = min(4, count // stride)
        vector = group_total(vector, axis, stride, size)
        stride *= size
    return vector


def pass_section(block_value, offset):
    return from_behind(block_value, "pipe", offset)


def keep_active(active, fresh_state, old_state):
    return jax.tree.map(lambda fresh, old: jnp.where(active, fresh, old), fresh_state, old_state)


def shards(tokens, norm_gains, qkv_weight, out_weight, cotangent):
    sections = lax.axis_size("pipe")
    section_index = lax.axis_index("pipe")
    qkv_cols = qkv_weight.shape[2]
    joined = jnp.concatenate([qkv_weight, out_weight], axis=2)
    joined_full = lax.all_gather(joined, "dp", axis=1, tiled=True)[0]
    qkv_local = joined_full[:, :qkv_cols]
    out_local = joined_full[:, qkv_cols:]
    gain_row = norm_gains[0]
    tokens_local = tokens[0]
    grads_local = cotangent[0]
    seq_len = tokens_local.shape[0]
    model_width = tokens_local.shape[1]
    proj_cols = qkv_local.shape[1]
    groups = proj_cols // ((GROUP + 2) * HD)
    head_cols = groups * GROUP * HD
    positions = jnp.arange(seq_len)
    contract_last = (((1,), (1,)), ((), ()))
    contract_rows = (((0,), (0,)), ((), ()))

    def forward_pass(block_in):
        normed, recip_rms, normed_low = norm_parts(block_in, gain_row)
        projected = lax.optimization_barrier(
            jnp.dot(normed_low, qkv_local, preferred_element_type=jnp.float32)
        ).reshape(seq_len, groups, GROUP + 2, HD)
        query_rows = projected[:, :, :GROUP].astype(jnp.bfloat16)
        key_rows = projected[:, :, GROUP].astype(jnp.bfloat16)
        value_rows = projected[:, :, GROUP + 1].astype(jnp.bfloat16)
        attn_probs, probs_low, mixed_rows = attend(
            query_rows, key_rows, value_rows, positions, positions
        )
        flat_mixed = mixed_rows.reshape(seq_len, head_cols)
        partial_rows = lax.dot_general(
            flat_mixed, out_local, contract_last, preferred_element_type=jnp.float32
        )
        summed_rows, offset = tensor_scatter(partial_rows)
        rows_in = lax.dynamic_slice_in_dim(block_in, offset, summed_rows.shape[0], 0)
        rows_out = (rows_in.astype(jnp.float32) + summed_rows.astype(jnp.float32)).astype(
            jnp.bfloat16
        )
        saved = (normed, recip_rms, normed_low, query_rows, key_rows, value_rows,
                 attn_probs, probs_low, flat_mixed)
        return rows_out, saved

    def backward_pass(grad_in, saved):
        (normed, recip_rms, normed_low, query_rows, key_rows, value_rows,
         attn_probs, probs_low, flat_mixed) = saved
        grad_mixed = (
            jnp.dot(grad_in, out_local, preferred_element_type=jnp.float32)
            .astype(jnp.bfloat16)
            .reshape(seq_len, groups, GROUP, HD)
        )
        grad_query, grad_key, grad_value = attend_back(
            query_rows, key_rows, value_rows, attn_probs, probs_low, grad_mixed
        )
        grad_proj = jnp.concatenate(
            [
                grad_query.astype(jnp.bfloat16),
                grad_key.astype(jnp.bfloat16)[:, :, None],
                grad_value.astype(jnp.bfloat16)[:, :, None],
            ],
            axis=2,
        ).reshape(seq_len, proj_cols)
        partial_rows = lax.dot_general(
            qkv_local, grad_proj, contract_last, preferred_element_type=jnp.float32
        ).T
        grad_rows, offset = tensor_scatter(partial_rows)
        count = grad_rows.shape[0]
        normed_rows = lax.dynamic_slice_in_dim(normed, offset, count, 0)
        recip_rows = lax.dynamic_slice_in_dim(recip_rms, offset, count, 0)
        grad_in_rows = lax.dynamic_slice_in_dim(grad_in, offset, count, 0)
        grad_float = grad_rows.astype(jnp.float32)
        scaled = grad_float * gain_row
        grad_norm_in = recip_rows * (
            scaled - normed_rows * jnp.mean(scaled * normed_rows, axis=-1, keepdims=True)
        )
        rows_out = (grad_in_rows.astype(jnp.float32) + grad_norm_in).astype(jnp.bfloat16)
        gain_part = jnp.sum(grad_float * normed_rows, axis=0)
        return rows_out, (grad_proj, gain_part)

    incoming = jnp.zeros_like(tokens_local)
    for turn in range(sections):
        block_in = jnp.where(section_index == 0, tokens_local, incoming)
        rows_out, saved = forward_pass(block_in)
        if turn < sections - 1:
            incoming = tensor_gather(pass_section(rows_out, 1))

    normed_low = saved[2]
    normed_cols = lax.all_to_all(normed_low, "dp", 1, 0, tiled=True)
    incoming = jnp.zeros_like(grads_local)
    for turn in range(sections):
        if turn == sections - 1:
            incoming, normed_cols = lax.optimization_barrier((incoming, normed_cols))
        grad_in = jnp.where(section_index == sections - 1, grads_local, incoming)
        rows_out, (grad_proj, gain_part) = backward_pass(grad_in, saved)
        if turn < sections - 1:
            incoming = tensor_gather(pass_section(rows_out, -1))

    normed_low = saved[2]
    flat_mixed = saved[8]
    seqs = lax.axis_size("dp")
    slice_width = model_width // seqs
    mixed_rows = lax.all_gather(flat_mixed, "dp", axis=0, tiled=True)
    grad_cols = lax.all_to_all(grad_in, "dp", 1, 0, tiled=True)
    dproj_rows = lax.all_gather(grad_proj, "dp", axis=0, tiled=True)
    qkv_result = lax.dot_general(
        normed_cols, dproj_rows, contract_rows, preferred_element_type=jnp.float32
    )[None]
    out_result = lax.dot_general(
        grad_cols, mixed_rows, contract_rows, preferred_element_type=jnp.float32
    )[None]
    gain_total = axis_total(axis_total(gain_part, "tensor"), "dp")
    gain_result = lax.dynamic_slice_in_dim(
        gain_total, lax.axis_index("dp") * slice_width, slice_width, 0
    )[None]
    return (qkv_result, out_result, gain_result)


def solution(mesh):
    in_specs = (
        P("dp", None, None),
        P("pipe", None),
        P("pipe", "dp", "tensor"),
        P("pipe", "dp", "tensor"),
        P("dp", None, None),
    )
    out_specs = (P("pipe", "dp", "tensor"), P("pipe", "dp", "tensor"), P("pipe", "dp"))
    return jax.shard_map(shards, mesh=mesh, in_specs=in_specs, out_specs=out_specs, check_vma=False)
```

```python
import jax
import jax.numpy as jnp
from jax import lax
from jax.sharding import PartitionSpec as P

HD = 128
GROUP = 4
BLOCK = 32


EPSILON = 1e-05
HIGH = lax.Precision.HIGHEST


def from_behind(value, axis, steps):
    count = lax.axis_size(axis)
    leading, last = (max(0, -steps), min(count, count - steps))
    return lax.ppermute(value, axis, [(source, source + steps) for source in range(leading, last)])


def norm_parts(block_rows, gain_row):
    values = block_rows.astype(jnp.float32)
    recip_rms = lax.rsqrt(jnp.mean(values * values, axis=-1, keepdims=True) + EPSILON)
    normed = values * recip_rms
    return (normed, recip_rms, (normed * gain_row).astype(jnp.bfloat16))


def attend(query_rows, key_rows, value_rows, query_pos, key_pos):
    score_scale = query_rows.shape[-1] ** (-0.5)
    scores = (
        jnp.einsum("rgjd,cgd->gjrc", query_rows, key_rows, preferred_element_type=jnp.float32)
        * score_scale
    )
    allowed = key_pos[None, :] <= query_pos[:, None]
    scores = jnp.where(allowed, scores, -jnp.inf)
    row_max = jnp.max(scores, axis=-1, keepdims=True)
    raised = jnp.exp(scores - row_max)
    attn_probs = raised / jnp.sum(raised, axis=-1, keepdims=True)
    probs_low = attn_probs.astype(jnp.bfloat16)
    mixed_rows = jnp.einsum(
        "gjrc,cgd->rgjd", probs_low, value_rows, preferred_element_type=jnp.float32
    )
    return (attn_probs, probs_low, mixed_rows.astype(jnp.bfloat16))


def attend_back(query_rows, key_rows, value_rows, attn_probs, probs_low, grad_mixed):
    score_scale = query_rows.shape[-1] ** (-0.5)
    grad_low = jnp.einsum(
        "rgjd,cgd->gjrc", grad_mixed, value_rows, preferred_element_type=jnp.float32
    )
    inner_sum = jnp.sum(attn_probs * grad_low, axis=-1, keepdims=True)
    grad_score = attn_probs * (grad_low - inner_sum) * score_scale
    grad_query = jnp.einsum(
        "gjrc,cgd->rgjd", grad_score, key_rows.astype(jnp.float32), precision=HIGH
    )
    grad_key = jnp.einsum(
        "gjrc,rgjd->cgd", grad_score, query_rows.astype(jnp.float32), precision=HIGH
    )
    grad_value = jnp.einsum(
        "gjrc,rgjd->cgd", probs_low, grad_mixed, preferred_element_type=jnp.float32
    )
    return (grad_query, grad_key, grad_value)


def exchange(value, axis, mask):
    count = lax.axis_size(axis)
    return lax.ppermute(value, axis, [(source, source ^ mask) for source in range(count)])


def tensor_scatter(partial_rows):
    count = lax.axis_size("tensor")
    member = lax.axis_index("tensor")
    values = partial_rows.astype(jnp.bfloat16)
    offset = 0
    mask = 1
    while mask < count:
        bit = (member // mask) % 2
        half = values.shape[0] // 2
        keep = lax.dynamic_slice_in_dim(values, bit * half, half, 0)
        give = lax.dynamic_slice_in_dim(values, (1 - bit) * half, half, 0)
        values = (
            keep.astype(jnp.float32) + exchange(give, "tensor", mask).astype(jnp.float32)
        ).astype(jnp.bfloat16)
        offset = offset + bit * half
        mask *= 2
    return values, offset


def tensor_gather(block):
    count = lax.axis_size("tensor")
    member = lax.axis_index("tensor")
    values = block
    mask = count // 2
    while mask >= 1:
        bit = (member // mask) % 2
        other = exchange(values, "tensor", mask)
        values = jnp.where(
            bit == 0,
            jnp.concatenate([values, other], axis=0),
            jnp.concatenate([other, values], axis=0),
        )
        mask //= 2
    return values


def tensor_total(vector):
    count = lax.axis_size("tensor")
    mask = 1
    while mask < count:
        vector = vector + exchange(vector, "tensor", mask)
        mask *= 2
    return vector


def group_total(vector, axis, stride, size):
    count = lax.axis_size(axis)
    member = lax.axis_index(axis)
    digit = (member // stride) % size

    def moved(source, shift):
        source_digit = (source // stride) % size
        return source + ((source_digit + shift) % size - source_digit) * stride

    received = [vector] + [
        lax.ppermute(vector, axis, [(source, moved(source, shift)) for source in range(count)])
        for shift in range(1, size)
    ]
    stacked = jnp.stack(received)
    ordered = [stacked[(digit - j) % size] for j in range(size)]
    while len(ordered) > 1:
        ordered = [ordered[i] + ordered[i + 1] for i in range(0, len(ordered), 2)]
    return ordered[0]


def axis_total(vector, axis):
    count = lax.axis_size(axis)
    stride = 1
    while stride < count:
        size = min(4, count // stride)
        vector = group_total(vector, axis, stride, size)
        stride *= size
    return vector


def pass_section(block_value, offset):
    return from_behind(block_value, "pipe", offset)


def keep_active(active, fresh_state, old_state):
    return jax.tree.map(lambda fresh, old: jnp.where(active, fresh, old), fresh_state, old_state)


def shards(tokens, norm_gains, qkv_weight, out_weight, cotangent):
    sections = lax.axis_size("pipe")
    section_index = lax.axis_index("pipe")
    qkv_cols = qkv_weight.shape[2]
    joined = jnp.concatenate([qkv_weight, out_weight], axis=2)
    joined_full = lax.all_gather(joined, "dp", axis=1, tiled=True)[0]
    qkv_local = joined_full[:, :qkv_cols]
    out_local = joined_full[:, qkv_cols:]
    gain_row = norm_gains[0]
    tokens_local = tokens[0]
    grads_local = cotangent[0]
    seq_len = tokens_local.shape[0]
    model_width = tokens_local.shape[1]
    proj_cols = qkv_local.shape[1]
    groups = proj_cols // ((GROUP + 2) * HD)
    head_cols = groups * GROUP * HD
    positions = jnp.arange(seq_len)
    contract_last = (((1,), (1,)), ((), ()))
    contract_rows = (((0,), (0,)), ((), ()))

    def forward_pass(block_in):
        normed, recip_rms, normed_low = norm_parts(block_in, gain_row)
        projected = lax.optimization_barrier(
            jnp.dot(normed_low, qkv_local, preferred_element_type=jnp.float32)
        ).reshape(seq_len, groups, GROUP + 2, HD)
        query_rows = projected[:, :, :GROUP].astype(jnp.bfloat16)
        key_rows = projected[:, :, GROUP].astype(jnp.bfloat16)
        value_rows = projected[:, :, GROUP + 1].astype(jnp.bfloat16)
        attn_probs, probs_low, mixed_rows = attend(
            query_rows, key_rows, value_rows, positions, positions
        )
        flat_mixed = mixed_rows.reshape(seq_len, head_cols)
        partial_rows = lax.dot_general(
            flat_mixed, out_local, contract_last, preferred_element_type=jnp.float32
        )
        summed_rows, offset = tensor_scatter(partial_rows)
        rows_in = lax.dynamic_slice_in_dim(block_in, offset, summed_rows.shape[0], 0)
        rows_out = (rows_in.astype(jnp.float32) + summed_rows.astype(jnp.float32)).astype(
            jnp.bfloat16
        )
        saved = (normed, recip_rms, normed_low, query_rows, key_rows, value_rows,
                 attn_probs, probs_low, flat_mixed)
        return rows_out, saved

    def backward_pass(grad_in, saved):
        (normed, recip_rms, normed_low, query_rows, key_rows, value_rows,
         attn_probs, probs_low, flat_mixed) = saved
        grad_mixed = (
            jnp.dot(grad_in, out_local, preferred_element_type=jnp.float32)
            .astype(jnp.bfloat16)
            .reshape(seq_len, groups, GROUP, HD)
        )
        grad_query, grad_key, grad_value = attend_back(
            query_rows, key_rows, value_rows, attn_probs, probs_low, grad_mixed
        )
        grad_proj = jnp.concatenate(
            [
                grad_query.astype(jnp.bfloat16),
                grad_key.astype(jnp.bfloat16)[:, :, None],
                grad_value.astype(jnp.bfloat16)[:, :, None],
            ],
            axis=2,
        ).reshape(seq_len, proj_cols)
        partial_rows = lax.dot_general(
            qkv_local, grad_proj, contract_last, preferred_element_type=jnp.float32
        ).T
        grad_rows, offset = tensor_scatter(partial_rows)
        count = grad_rows.shape[0]
        normed_rows = lax.dynamic_slice_in_dim(normed, offset, count, 0)
        recip_rows = lax.dynamic_slice_in_dim(recip_rms, offset, count, 0)
        grad_in_rows = lax.dynamic_slice_in_dim(grad_in, offset, count, 0)
        grad_float = grad_rows.astype(jnp.float32)
        scaled = grad_float * gain_row
        grad_norm_in = recip_rows * (
            scaled - normed_rows * jnp.mean(scaled * normed_rows, axis=-1, keepdims=True)
        )
        rows_out = (grad_in_rows.astype(jnp.float32) + grad_norm_in).astype(jnp.bfloat16)
        gain_part = jnp.sum(grad_float * normed_rows, axis=0)
        return rows_out, (grad_proj, gain_part)

    incoming = jnp.zeros_like(tokens_local)
    for turn in range(sections):
        block_in = jnp.where(section_index == 0, tokens_local, incoming)
        rows_out, saved = forward_pass(block_in)
        if turn < sections - 1:
            incoming = tensor_gather(pass_section(rows_out, 1))

    incoming = jnp.zeros_like(grads_local)
    for turn in range(sections):
        grad_in = jnp.where(section_index == sections - 1, grads_local, incoming)
        rows_out, (grad_proj, gain_part) = backward_pass(grad_in, saved)
        if turn < sections - 1:
            incoming = tensor_gather(pass_section(rows_out, -1))

    normed_low = saved[2]
    flat_mixed = saved[8]
    seqs = lax.axis_size("dp")
    slice_width = model_width // seqs
    mixed_rows = lax.all_gather(flat_mixed, "dp", axis=0, tiled=True)
    both_cols = lax.all_to_all(
        jnp.concatenate([normed_low, grad_in], axis=0), "dp", 1, 0, tiled=True
    ).reshape(seqs, 2, seq_len, slice_width)
    normed_cols = both_cols[:, 0].reshape(seqs * seq_len, slice_width)
    grad_cols = both_cols[:, 1].reshape(seqs * seq_len, slice_width)
    dproj_rows = lax.all_gather(grad_proj, "dp", axis=0, tiled=True)
    qkv_result = lax.dot_general(
        normed_cols, dproj_rows, contract_rows, preferred_element_type=jnp.float32
    )[None]
    out_result = lax.dot_general(
        grad_cols, mixed_rows, contract_rows, preferred_element_type=jnp.float32
    )[None]
    gain_total = axis_total(axis_total(gain_part, "tensor"), "dp")
    gain_result = lax.dynamic_slice_in_dim(
        gain_total, lax.axis_index("dp") * slice_width, slice_width, 0
    )[None]
    return (qkv_result, out_result, gain_result)


def solution(mesh):
    in_specs = (
        P("dp", None, None),
        P("pipe", None),
        P("pipe", "dp", "tensor"),
        P("pipe", "dp", "tensor"),
        P("dp", None, None),
    )
    out_specs = (P("pipe", "dp", "tensor"), P("pipe", "dp", "tensor"), P("pipe", "dp"))
    return jax.shard_map(shards, mesh=mesh, in_specs=in_specs, out_specs=out_specs, check_vma=False)
```

```python
import jax
import jax.numpy as jnp
from jax import lax
from jax.sharding import PartitionSpec as P

HD = 128
GROUP = 4
BLOCK = 32


EPSILON = 1e-05
HIGH = lax.Precision.HIGHEST


def from_behind(value, axis, steps):
    count = lax.axis_size(axis)
    leading, last = (max(0, -steps), min(count, count - steps))
    return lax.ppermute(value, axis, [(source, source + steps) for source in range(leading, last)])


def norm_parts(block_rows, gain_row):
    values = block_rows.astype(jnp.float32)
    recip_rms = lax.rsqrt(jnp.mean(values * values, axis=-1, keepdims=True) + EPSILON)
    normed = values * recip_rms
    return (normed, recip_rms, (normed * gain_row).astype(jnp.bfloat16))


def attend(query_rows, key_rows, value_rows, query_pos, key_pos):
    score_scale = query_rows.shape[-1] ** (-0.5)
    scores = (
        jnp.einsum("rgjd,cgd->gjrc", query_rows, key_rows, preferred_element_type=jnp.float32)
        * score_scale
    )
    allowed = key_pos[None, :] <= query_pos[:, None]
    scores = jnp.where(allowed, scores, -jnp.inf)
    row_max = jnp.max(scores, axis=-1, keepdims=True)
    raised = jnp.exp(scores - row_max)
    attn_probs = raised / jnp.sum(raised, axis=-1, keepdims=True)
    probs_low = attn_probs.astype(jnp.bfloat16)
    mixed_rows = jnp.einsum(
        "gjrc,cgd->rgjd", probs_low, value_rows, preferred_element_type=jnp.float32
    )
    return (attn_probs, probs_low, mixed_rows.astype(jnp.bfloat16))


def attend_back(query_rows, key_rows, value_rows, attn_probs, probs_low, grad_mixed):
    score_scale = query_rows.shape[-1] ** (-0.5)
    grad_low = jnp.einsum(
        "rgjd,cgd->gjrc", grad_mixed, value_rows, preferred_element_type=jnp.float32
    )
    inner_sum = jnp.sum(attn_probs * grad_low, axis=-1, keepdims=True)
    grad_score = attn_probs * (grad_low - inner_sum) * score_scale
    grad_query = jnp.einsum(
        "gjrc,cgd->rgjd", grad_score, key_rows.astype(jnp.float32), precision=HIGH
    )
    grad_key = jnp.einsum(
        "gjrc,rgjd->cgd", grad_score, query_rows.astype(jnp.float32), precision=HIGH
    )
    grad_value = jnp.einsum(
        "gjrc,rgjd->cgd", probs_low, grad_mixed, preferred_element_type=jnp.float32
    )
    return (grad_query, grad_key, grad_value)


def exchange(value, axis, mask):
    count = lax.axis_size(axis)
    return lax.ppermute(value, axis, [(source, source ^ mask) for source in range(count)])


def tensor_scatter(partial_rows):
    count = lax.axis_size("tensor")
    member = lax.axis_index("tensor")
    values = partial_rows.astype(jnp.bfloat16)
    offset = 0
    mask = 1
    while mask < count:
        bit = (member // mask) % 2
        half = values.shape[0] // 2
        keep = lax.dynamic_slice_in_dim(values, bit * half, half, 0)
        give = lax.dynamic_slice_in_dim(values, (1 - bit) * half, half, 0)
        values = (
            keep.astype(jnp.float32) + exchange(give, "tensor", mask).astype(jnp.float32)
        ).astype(jnp.bfloat16)
        offset = offset + bit * half
        mask *= 2
    return values, offset


def tensor_gather(block):
    count = lax.axis_size("tensor")
    member = lax.axis_index("tensor")
    values = block
    mask = count // 2
    while mask >= 1:
        bit = (member // mask) % 2
        other = exchange(values, "tensor", mask)
        values = jnp.where(
            bit == 0,
            jnp.concatenate([values, other], axis=0),
            jnp.concatenate([other, values], axis=0),
        )
        mask //= 2
    return values


def tensor_total(vector):
    count = lax.axis_size("tensor")
    mask = 1
    while mask < count:
        vector = vector + exchange(vector, "tensor", mask)
        mask *= 2
    return vector


def group_total(vector, axis, stride, size):
    count = lax.axis_size(axis)
    member = lax.axis_index(axis)
    digit = (member // stride) % size

    def moved(source, shift):
        source_digit = (source // stride) % size
        return source + ((source_digit + shift) % size - source_digit) * stride

    received = [vector] + [
        lax.ppermute(vector, axis, [(source, moved(source, shift)) for source in range(count)])
        for shift in range(1, size)
    ]
    stacked = jnp.stack(received)
    ordered = [stacked[(digit - j) % size] for j in range(size)]
    while len(ordered) > 1:
        ordered = [ordered[i] + ordered[i + 1] for i in range(0, len(ordered), 2)]
    return ordered[0]


def axis_total(vector, axis):
    count = lax.axis_size(axis)
    stride = 1
    while stride < count:
        size = min(4, count // stride)
        vector = group_total(vector, axis, stride, size)
        stride *= size
    return vector


def pass_section(block_value, offset):
    return from_behind(block_value, "pipe", offset)


def keep_active(active, fresh_state, old_state):
    return jax.tree.map(lambda fresh, old: jnp.where(active, fresh, old), fresh_state, old_state)


def shards(tokens, norm_gains, qkv_weight, out_weight, cotangent):
    sections = lax.axis_size("pipe")
    section_index = lax.axis_index("pipe")
    qkv_cols = qkv_weight.shape[2]
    joined = jnp.concatenate([qkv_weight, out_weight], axis=2)
    joined_full = lax.all_gather(joined, "dp", axis=1, tiled=True)[0]
    qkv_local = joined_full[:, :qkv_cols]
    out_local = joined_full[:, qkv_cols:]
    gain_row = norm_gains[0]
    tokens_local = tokens[0]
    grads_local = cotangent[0]
    seq_len = tokens_local.shape[0]
    model_width = tokens_local.shape[1]
    proj_cols = qkv_local.shape[1]
    groups = proj_cols // ((GROUP + 2) * HD)
    head_cols = groups * GROUP * HD
    positions = jnp.arange(seq_len)
    contract_last = (((1,), (1,)), ((), ()))
    contract_rows = (((0,), (0,)), ((), ()))

    def forward_pass(block_in):
        normed, recip_rms, normed_low = norm_parts(block_in, gain_row)
        projected = lax.optimization_barrier(
            jnp.dot(normed_low, qkv_local, preferred_element_type=jnp.float32)
        ).reshape(seq_len, groups, GROUP + 2, HD)
        query_rows = projected[:, :, :GROUP].astype(jnp.bfloat16)
        key_rows = projected[:, :, GROUP].astype(jnp.bfloat16)
        value_rows = projected[:, :, GROUP + 1].astype(jnp.bfloat16)
        attn_probs, probs_low, mixed_rows = attend(
            query_rows, key_rows, value_rows, positions, positions
        )
        flat_mixed = mixed_rows.reshape(seq_len, head_cols)
        partial_rows = lax.dot_general(
            flat_mixed, out_local, contract_last, preferred_element_type=jnp.float32
        )
        summed_rows, offset = tensor_scatter(partial_rows)
        rows_in = lax.dynamic_slice_in_dim(block_in, offset, summed_rows.shape[0], 0)
        rows_out = (rows_in.astype(jnp.float32) + summed_rows.astype(jnp.float32)).astype(
            jnp.bfloat16
        )
        saved = (normed, recip_rms, normed_low, query_rows, key_rows, value_rows,
                 attn_probs, probs_low, flat_mixed)
        return rows_out, saved

    def backward_pass(grad_in, saved):
        (normed, recip_rms, normed_low, query_rows, key_rows, value_rows,
         attn_probs, probs_low, flat_mixed) = saved
        grad_mixed = (
            jnp.dot(grad_in, out_local, preferred_element_type=jnp.float32)
            .astype(jnp.bfloat16)
            .reshape(seq_len, groups, GROUP, HD)
        )
        grad_query, grad_key, grad_value = attend_back(
            query_rows, key_rows, value_rows, attn_probs, probs_low, grad_mixed
        )
        grad_proj = jnp.concatenate(
            [
                grad_query.astype(jnp.bfloat16),
                grad_key.astype(jnp.bfloat16)[:, :, None],
                grad_value.astype(jnp.bfloat16)[:, :, None],
            ],
            axis=2,
        ).reshape(seq_len, proj_cols)
        partial_rows = lax.dot_general(
            qkv_local, grad_proj, contract_last, preferred_element_type=jnp.float32
        ).T
        grad_rows, offset = tensor_scatter(partial_rows)
        count = grad_rows.shape[0]
        normed_rows = lax.dynamic_slice_in_dim(normed, offset, count, 0)
        recip_rows = lax.dynamic_slice_in_dim(recip_rms, offset, count, 0)
        grad_in_rows = lax.dynamic_slice_in_dim(grad_in, offset, count, 0)
        grad_float = grad_rows.astype(jnp.float32)
        scaled = grad_float * gain_row
        grad_norm_in = recip_rows * (
            scaled - normed_rows * jnp.mean(scaled * normed_rows, axis=-1, keepdims=True)
        )
        rows_out = (grad_in_rows.astype(jnp.float32) + grad_norm_in).astype(jnp.bfloat16)
        gain_part = jnp.sum(grad_float * normed_rows, axis=0)
        return rows_out, (grad_proj, gain_part)

    incoming = jnp.zeros_like(tokens_local)
    for turn in range(sections):
        block_in = jnp.where(section_index == 0, tokens_local, incoming)
        rows_out, saved = forward_pass(block_in)
        if turn < sections - 1:
            incoming = tensor_gather(pass_section(rows_out, 1))

    incoming = jnp.zeros_like(grads_local)
    for turn in range(sections):
        grad_in = jnp.where(section_index == sections - 1, grads_local, incoming)
        rows_out, (grad_proj, gain_part) = backward_pass(grad_in, saved)
        if turn < sections - 1:
            incoming = tensor_gather(pass_section(rows_out, -1))

    normed_low = saved[2]
    flat_mixed = saved[8]
    seqs = lax.axis_size("dp")
    slice_width = model_width // seqs
    mixed_rows = lax.all_gather(flat_mixed, "dp", axis=0, tiled=True)
    gain_rows = 8
    gain_seq = axis_total(gain_part, "tensor")
    gain_block = jnp.zeros((gain_rows, model_width), jnp.bfloat16).at[0].set(gain_seq.astype(jnp.bfloat16))
    block_rows = 2 * seq_len + gain_rows
    both_cols = lax.all_to_all(
        jnp.concatenate([normed_low, grad_in, gain_block], axis=0), "dp", 1, 0, tiled=True
    ).reshape(seqs, block_rows, slice_width)
    normed_cols = both_cols[:, :seq_len].reshape(seqs * seq_len, slice_width)
    grad_cols = both_cols[:, seq_len : 2 * seq_len].reshape(seqs * seq_len, slice_width)
    gain_slices = both_cols[:, 2 * seq_len].astype(jnp.float32)
    dproj_rows = lax.all_gather(grad_proj, "dp", axis=0, tiled=True)
    qkv_result = lax.dot_general(
        normed_cols, dproj_rows, contract_rows, preferred_element_type=jnp.float32
    )[None]
    out_result = lax.dot_general(
        grad_cols, mixed_rows, contract_rows, preferred_element_type=jnp.float32
    )[None]
    gain_result = jnp.sum(gain_slices, axis=0)[None]
    return (qkv_result, out_result, gain_result)


def solution(mesh):
    in_specs = (
        P("dp", None, None),
        P("pipe", None),
        P("pipe", "dp", "tensor"),
        P("pipe", "dp", "tensor"),
        P("dp", None, None),
    )
    out_specs = (P("pipe", "dp", "tensor"), P("pipe", "dp", "tensor"), P("pipe", "dp"))
    return jax.shard_map(shards, mesh=mesh, in_specs=in_specs, out_specs=out_specs, check_vma=False)
```

```python
import jax
import jax.numpy as jnp
from jax import lax
from jax.sharding import PartitionSpec as P

HD = 128
GROUP = 4
BLOCK = 32


EPSILON = 1e-05
HIGH = lax.Precision.HIGHEST


def from_behind(value, axis, steps):
    count = lax.axis_size(axis)
    leading, last = (max(0, -steps), min(count, count - steps))
    return lax.ppermute(value, axis, [(source, source + steps) for source in range(leading, last)])


def norm_parts(block_rows, gain_row):
    values = block_rows.astype(jnp.float32)
    recip_rms = lax.rsqrt(jnp.mean(values * values, axis=-1, keepdims=True) + EPSILON)
    normed = values * recip_rms
    return (normed, recip_rms, (normed * gain_row).astype(jnp.bfloat16))


def attend(query_rows, key_rows, value_rows, query_pos, key_pos):
    score_scale = query_rows.shape[-1] ** (-0.5)
    scores = (
        jnp.einsum("rgjd,cgd->gjrc", query_rows, key_rows, preferred_element_type=jnp.float32)
        * score_scale
    )
    allowed = key_pos[None, :] <= query_pos[:, None]
    scores = jnp.where(allowed, scores, -jnp.inf)
    row_max = jnp.max(scores, axis=-1, keepdims=True)
    raised = jnp.exp(scores - row_max)
    attn_probs = raised / jnp.sum(raised, axis=-1, keepdims=True)
    probs_low = attn_probs.astype(jnp.bfloat16)
    mixed_rows = jnp.einsum(
        "gjrc,cgd->rgjd", probs_low, value_rows, preferred_element_type=jnp.float32
    )
    return (attn_probs, probs_low, mixed_rows.astype(jnp.bfloat16))


def attend_back(query_rows, key_rows, value_rows, attn_probs, probs_low, grad_mixed):
    score_scale = query_rows.shape[-1] ** (-0.5)
    grad_low = jnp.einsum(
        "rgjd,cgd->gjrc", grad_mixed, value_rows, preferred_element_type=jnp.float32
    )
    inner_sum = jnp.sum(attn_probs * grad_low, axis=-1, keepdims=True)
    grad_score = attn_probs * (grad_low - inner_sum) * score_scale
    grad_query = jnp.einsum(
        "gjrc,cgd->rgjd", grad_score, key_rows.astype(jnp.float32), precision=HIGH
    )
    grad_key = jnp.einsum(
        "gjrc,rgjd->cgd", grad_score, query_rows.astype(jnp.float32), precision=HIGH
    )
    grad_value = jnp.einsum(
        "gjrc,rgjd->cgd", probs_low, grad_mixed, preferred_element_type=jnp.float32
    )
    return (grad_query, grad_key, grad_value)


def exchange(value, axis, mask):
    count = lax.axis_size(axis)
    return lax.ppermute(value, axis, [(source, source ^ mask) for source in range(count)])


def tensor_scatter(partial_rows):
    count = lax.axis_size("tensor")
    member = lax.axis_index("tensor")
    values = partial_rows.astype(jnp.bfloat16)
    offset = 0
    mask = 1
    while mask < count:
        bit = (member // mask) % 2
        half = values.shape[0] // 2
        keep = lax.dynamic_slice_in_dim(values, bit * half, half, 0)
        give = lax.dynamic_slice_in_dim(values, (1 - bit) * half, half, 0)
        values = (
            keep.astype(jnp.float32) + exchange(give, "tensor", mask).astype(jnp.float32)
        ).astype(jnp.bfloat16)
        offset = offset + bit * half
        mask *= 2
    return values, offset


def tensor_gather(block):
    count = lax.axis_size("tensor")
    member = lax.axis_index("tensor")
    values = block
    mask = count // 2
    while mask >= 1:
        bit = (member // mask) % 2
        other = exchange(values, "tensor", mask)
        values = jnp.where(
            bit == 0,
            jnp.concatenate([values, other], axis=0),
            jnp.concatenate([other, values], axis=0),
        )
        mask //= 2
    return values


def tensor_total(vector):
    count = lax.axis_size("tensor")
    mask = 1
    while mask < count:
        vector = vector + exchange(vector, "tensor", mask)
        mask *= 2
    return vector


def group_total(vector, axis, stride, size):
    count = lax.axis_size(axis)
    member = lax.axis_index(axis)
    digit = (member // stride) % size

    def moved(source, shift):
        source_digit = (source // stride) % size
        return source + ((source_digit + shift) % size - source_digit) * stride

    received = [vector] + [
        lax.ppermute(vector, axis, [(source, moved(source, shift)) for source in range(count)])
        for shift in range(1, size)
    ]
    stacked = jnp.stack(received)
    ordered = [stacked[(digit - j) % size] for j in range(size)]
    while len(ordered) > 1:
        ordered = [ordered[i] + ordered[i + 1] for i in range(0, len(ordered), 2)]
    return ordered[0]


def group_gather(block, axis, stride, size):
    count = lax.axis_size(axis)
    member = lax.axis_index(axis)
    digit = (member // stride) % size

    def moved(source, shift):
        source_digit = (source // stride) % size
        return source + ((source_digit + shift) % size - source_digit) * stride

    received = [block] + [
        lax.ppermute(block, axis, [(source, moved(source, shift)) for source in range(count)])
        for shift in range(1, size)
    ]
    stacked = jnp.stack(received)
    return jnp.stack([stacked[(digit - j) % size] for j in range(size)])


def axis_gather(block, axis):
    count = lax.axis_size(axis)
    stride = 1
    values = block
    while stride < count:
        size = min(4, count // stride)
        values = group_gather(values, axis, stride, size)
        stride *= size
    return values.reshape((count,) + block.shape)


def axis_total(vector, axis):
    count = lax.axis_size(axis)
    stride = 1
    while stride < count:
        size = min(4, count // stride)
        vector = group_total(vector, axis, stride, size)
        stride *= size
    return vector


def pass_section(block_value, offset):
    return from_behind(block_value, "pipe", offset)


def keep_active(active, fresh_state, old_state):
    return jax.tree.map(lambda fresh, old: jnp.where(active, fresh, old), fresh_state, old_state)


def shards(tokens, norm_gains, qkv_weight, out_weight, cotangent):
    sections = lax.axis_size("pipe")
    section_index = lax.axis_index("pipe")
    qkv_cols = qkv_weight.shape[2]
    joined = jnp.concatenate([qkv_weight, out_weight], axis=2)
    joined_full = lax.all_gather(joined, "dp", axis=1, tiled=True)[0]
    qkv_local = joined_full[:, :qkv_cols]
    out_local = joined_full[:, qkv_cols:]
    gain_row = norm_gains[0]
    tokens_local = tokens[0]
    grads_local = cotangent[0]
    seq_len = tokens_local.shape[0]
    model_width = tokens_local.shape[1]
    proj_cols = qkv_local.shape[1]
    groups = proj_cols // ((GROUP + 2) * HD)
    head_cols = groups * GROUP * HD
    positions = jnp.arange(seq_len)
    contract_last = (((1,), (1,)), ((), ()))
    contract_rows = (((0,), (0,)), ((), ()))

    def forward_pass(block_in):
        normed, recip_rms, normed_low = norm_parts(block_in, gain_row)
        projected = lax.optimization_barrier(
            jnp.dot(normed_low, qkv_local, preferred_element_type=jnp.float32)
        ).reshape(seq_len, groups, GROUP + 2, HD)
        query_rows = projected[:, :, :GROUP].astype(jnp.bfloat16)
        key_rows = projected[:, :, GROUP].astype(jnp.bfloat16)
        value_rows = projected[:, :, GROUP + 1].astype(jnp.bfloat16)
        attn_probs, probs_low, mixed_rows = attend(
            query_rows, key_rows, value_rows, positions, positions
        )
        flat_mixed = mixed_rows.reshape(seq_len, head_cols)
        partial_rows = lax.dot_general(
            flat_mixed, out_local, contract_last, preferred_element_type=jnp.float32
        )
        summed_rows, offset = tensor_scatter(partial_rows)
        rows_in = lax.dynamic_slice_in_dim(block_in, offset, summed_rows.shape[0], 0)
        rows_out = (rows_in.astype(jnp.float32) + summed_rows.astype(jnp.float32)).astype(
            jnp.bfloat16
        )
        saved = (normed, recip_rms, normed_low, query_rows, key_rows, value_rows,
                 attn_probs, probs_low, flat_mixed)
        return rows_out, saved

    def backward_pass(grad_in, saved):
        (normed, recip_rms, normed_low, query_rows, key_rows, value_rows,
         attn_probs, probs_low, flat_mixed) = saved
        grad_mixed = (
            jnp.dot(grad_in, out_local, preferred_element_type=jnp.float32)
            .astype(jnp.bfloat16)
            .reshape(seq_len, groups, GROUP, HD)
        )
        grad_query, grad_key, grad_value = attend_back(
            query_rows, key_rows, value_rows, attn_probs, probs_low, grad_mixed
        )
        grad_proj = jnp.concatenate(
            [
                grad_query.astype(jnp.bfloat16),
                grad_key.astype(jnp.bfloat16)[:, :, None],
                grad_value.astype(jnp.bfloat16)[:, :, None],
            ],
            axis=2,
        ).reshape(seq_len, proj_cols)
        partial_rows = lax.dot_general(
            qkv_local, grad_proj, contract_last, preferred_element_type=jnp.float32
        ).T
        grad_rows, offset = tensor_scatter(partial_rows)
        count = grad_rows.shape[0]
        normed_rows = lax.dynamic_slice_in_dim(normed, offset, count, 0)
        recip_rows = lax.dynamic_slice_in_dim(recip_rms, offset, count, 0)
        grad_in_rows = lax.dynamic_slice_in_dim(grad_in, offset, count, 0)
        grad_float = grad_rows.astype(jnp.float32)
        scaled = grad_float * gain_row
        grad_norm_in = recip_rows * (
            scaled - normed_rows * jnp.mean(scaled * normed_rows, axis=-1, keepdims=True)
        )
        rows_out = (grad_in_rows.astype(jnp.float32) + grad_norm_in).astype(jnp.bfloat16)
        gain_part = jnp.sum(grad_float * normed_rows, axis=0)
        return rows_out, (grad_proj, gain_part)

    incoming = jnp.zeros_like(tokens_local)
    for turn in range(sections):
        block_in = jnp.where(section_index == 0, tokens_local, incoming)
        rows_out, saved = forward_pass(block_in)
        if turn < sections - 1:
            incoming = tensor_gather(pass_section(rows_out, 1))

    incoming = jnp.zeros_like(grads_local)
    for turn in range(sections):
        grad_in = jnp.where(section_index == sections - 1, grads_local, incoming)
        rows_out, (grad_proj, gain_part) = backward_pass(grad_in, saved)
        if turn < sections - 1:
            incoming = tensor_gather(pass_section(rows_out, -1))

    normed_low = saved[2]
    flat_mixed = saved[8]
    seqs = lax.axis_size("dp")
    slice_width = model_width // seqs
    mixed_rows = lax.all_gather(flat_mixed, "dp", axis=0, tiled=True)
    gain_rows = 8
    gain_seq = axis_total(gain_part, "tensor")
    gain_block = jnp.zeros((gain_rows, model_width), jnp.bfloat16).at[0].set(gain_seq.astype(jnp.bfloat16))
    block_rows = 2 * seq_len + gain_rows
    both_cols = lax.all_to_all(
        jnp.concatenate([normed_low, grad_in, gain_block], axis=0), "dp", 1, 0, tiled=True
    ).reshape(seqs, block_rows, slice_width)
    normed_cols = both_cols[:, :seq_len].reshape(seqs * seq_len, slice_width)
    grad_cols = both_cols[:, seq_len : 2 * seq_len].reshape(seqs * seq_len, slice_width)
    gain_slices = both_cols[:, 2 * seq_len].astype(jnp.float32)
    split_rows = seq_len // 2
    dproj_first = lax.all_gather(grad_proj[:split_rows], "dp", axis=0, tiled=True)
    dproj_second = axis_gather(grad_proj[split_rows:], "dp").reshape(seqs * split_rows, proj_cols)
    normed_split = normed_cols.reshape(seqs, seq_len, slice_width)
    normed_first = normed_split[:, :split_rows].reshape(seqs * split_rows, slice_width)
    normed_second = normed_split[:, split_rows:].reshape(seqs * split_rows, slice_width)
    qkv_result = (
        lax.dot_general(normed_first, dproj_first, contract_rows, preferred_element_type=jnp.float32)
        + lax.dot_general(
            normed_second, dproj_second, contract_rows, preferred_element_type=jnp.float32
        )
    )[None]
    out_result = lax.dot_general(
        grad_cols, mixed_rows, contract_rows, preferred_element_type=jnp.float32
    )[None]
    gain_result = jnp.sum(gain_slices, axis=0)[None]
    return (qkv_result, out_result, gain_result)


def solution(mesh):
    in_specs = (
        P("dp", None, None),
        P("pipe", None),
        P("pipe", "dp", "tensor"),
        P("pipe", "dp", "tensor"),
        P("dp", None, None),
    )
    out_specs = (P("pipe", "dp", "tensor"), P("pipe", "dp", "tensor"), P("pipe", "dp"))
    return jax.shard_map(shards, mesh=mesh, in_specs=in_specs, out_specs=out_specs, check_vma=False)
```

```python
import jax
import jax.numpy as jnp
from jax import lax
from jax.sharding import PartitionSpec as P

HD = 128
GROUP = 4
BLOCK = 32


EPSILON = 1e-05
HIGH = lax.Precision.HIGHEST


def from_behind(value, axis, steps):
    count = lax.axis_size(axis)
    leading, last = (max(0, -steps), min(count, count - steps))
    return lax.ppermute(value, axis, [(source, source + steps) for source in range(leading, last)])


def norm_parts(block_rows, gain_row):
    values = block_rows.astype(jnp.float32)
    recip_rms = lax.rsqrt(jnp.mean(values * values, axis=-1, keepdims=True) + EPSILON)
    normed = values * recip_rms
    return (normed, recip_rms, (normed * gain_row).astype(jnp.bfloat16))


def attend(query_rows, key_rows, value_rows, query_pos, key_pos):
    score_scale = query_rows.shape[-1] ** (-0.5)
    scores = (
        jnp.einsum("rgjd,cgd->gjrc", query_rows, key_rows, preferred_element_type=jnp.float32)
        * score_scale
    )
    allowed = key_pos[None, :] <= query_pos[:, None]
    scores = jnp.where(allowed, scores, -jnp.inf)
    row_max = jnp.max(scores, axis=-1, keepdims=True)
    raised = jnp.exp(scores - row_max)
    attn_probs = raised / jnp.sum(raised, axis=-1, keepdims=True)
    probs_low = attn_probs.astype(jnp.bfloat16)
    mixed_rows = jnp.einsum(
        "gjrc,cgd->rgjd", probs_low, value_rows, preferred_element_type=jnp.float32
    )
    return (attn_probs, probs_low, mixed_rows.astype(jnp.bfloat16))


def attend_back(query_rows, key_rows, value_rows, attn_probs, probs_low, grad_mixed):
    score_scale = query_rows.shape[-1] ** (-0.5)
    grad_low = jnp.einsum(
        "rgjd,cgd->gjrc", grad_mixed, value_rows, preferred_element_type=jnp.float32
    )
    inner_sum = jnp.sum(attn_probs * grad_low, axis=-1, keepdims=True)
    grad_score = attn_probs * (grad_low - inner_sum) * score_scale
    grad_query = jnp.einsum(
        "gjrc,cgd->rgjd", grad_score, key_rows.astype(jnp.float32), precision=HIGH
    )
    grad_key = jnp.einsum(
        "gjrc,rgjd->cgd", grad_score, query_rows.astype(jnp.float32), precision=HIGH
    )
    grad_value = jnp.einsum(
        "gjrc,rgjd->cgd", probs_low, grad_mixed, preferred_element_type=jnp.float32
    )
    return (grad_query, grad_key, grad_value)


def exchange(value, axis, mask):
    count = lax.axis_size(axis)
    return lax.ppermute(value, axis, [(source, source ^ mask) for source in range(count)])


def tensor_scatter(partial_rows):
    count = lax.axis_size("tensor")
    member = lax.axis_index("tensor")
    values = partial_rows.astype(jnp.bfloat16)
    offset = 0
    mask = 1
    while mask < count:
        bit = (member // mask) % 2
        half = values.shape[0] // 2
        keep = lax.dynamic_slice_in_dim(values, bit * half, half, 0)
        give = lax.dynamic_slice_in_dim(values, (1 - bit) * half, half, 0)
        values = (
            keep.astype(jnp.float32) + exchange(give, "tensor", mask).astype(jnp.float32)
        ).astype(jnp.bfloat16)
        offset = offset + bit * half
        mask *= 2
    return values, offset


def tensor_gather(block, flip=0):
    count = lax.axis_size("tensor")
    member = lax.axis_index("tensor")
    values = block
    mask = count // 2
    while mask >= 1:
        bit = ((member ^ flip) // mask) % 2
        other = exchange(values, "tensor", mask)
        values = jnp.where(
            bit == 0,
            jnp.concatenate([values, other], axis=0),
            jnp.concatenate([other, values], axis=0),
        )
        mask //= 2
    return values


def tensor_total(vector):
    count = lax.axis_size("tensor")
    mask = 1
    while mask < count:
        vector = vector + exchange(vector, "tensor", mask)
        mask *= 2
    return vector


def group_total(vector, axis, stride, size):
    count = lax.axis_size(axis)
    member = lax.axis_index(axis)
    digit = (member // stride) % size

    def moved(source, shift):
        source_digit = (source // stride) % size
        return source + ((source_digit + shift) % size - source_digit) * stride

    received = [vector] + [
        lax.ppermute(vector, axis, [(source, moved(source, shift)) for source in range(count)])
        for shift in range(1, size)
    ]
    stacked = jnp.stack(received)
    ordered = [stacked[(digit - j) % size] for j in range(size)]
    while len(ordered) > 1:
        ordered = [ordered[i] + ordered[i + 1] for i in range(0, len(ordered), 2)]
    return ordered[0]


def axis_total(vector, axis):
    count = lax.axis_size(axis)
    stride = 1
    while stride < count:
        size = min(4, count // stride)
        vector = group_total(vector, axis, stride, size)
        stride *= size
    return vector


def relay_flip():
    return lax.axis_size("tensor") // 2


def pass_section(block_value, offset):
    sections = lax.axis_size("pipe")
    members = lax.axis_size("tensor")
    flip = relay_flip()
    pairs = [
        (source * members + member, (source + offset) * members + (member ^ flip))
        for source in range(sections)
        if 0 <= source + offset < sections
        for member in range(members)
    ]
    return lax.ppermute(block_value, ("pipe", "tensor"), pairs)


def keep_active(active, fresh_state, old_state):
    return jax.tree.map(lambda fresh, old: jnp.where(active, fresh, old), fresh_state, old_state)


def shards(tokens, norm_gains, qkv_weight, out_weight, cotangent):
    sections = lax.axis_size("pipe")
    section_index = lax.axis_index("pipe")
    qkv_cols = qkv_weight.shape[2]
    joined = jnp.concatenate([qkv_weight, out_weight], axis=2)
    joined_full = lax.all_gather(joined, "dp", axis=1, tiled=True)[0]
    qkv_local = joined_full[:, :qkv_cols]
    out_local = joined_full[:, qkv_cols:]
    gain_row = norm_gains[0]
    tokens_local = tokens[0]
    grads_local = cotangent[0]
    seq_len = tokens_local.shape[0]
    model_width = tokens_local.shape[1]
    proj_cols = qkv_local.shape[1]
    groups = proj_cols // ((GROUP + 2) * HD)
    head_cols = groups * GROUP * HD
    positions = jnp.arange(seq_len)
    contract_last = (((1,), (1,)), ((), ()))
    contract_rows = (((0,), (0,)), ((), ()))

    def forward_pass(block_in):
        normed, recip_rms, normed_low = norm_parts(block_in, gain_row)
        projected = lax.optimization_barrier(
            jnp.dot(normed_low, qkv_local, preferred_element_type=jnp.float32)
        ).reshape(seq_len, groups, GROUP + 2, HD)
        query_rows = projected[:, :, :GROUP].astype(jnp.bfloat16)
        key_rows = projected[:, :, GROUP].astype(jnp.bfloat16)
        value_rows = projected[:, :, GROUP + 1].astype(jnp.bfloat16)
        attn_probs, probs_low, mixed_rows = attend(
            query_rows, key_rows, value_rows, positions, positions
        )
        flat_mixed = mixed_rows.reshape(seq_len, head_cols)
        partial_rows = lax.dot_general(
            flat_mixed, out_local, contract_last, preferred_element_type=jnp.float32
        )
        summed_rows, offset = tensor_scatter(partial_rows)
        rows_in = lax.dynamic_slice_in_dim(block_in, offset, summed_rows.shape[0], 0)
        rows_out = (rows_in.astype(jnp.float32) + summed_rows.astype(jnp.float32)).astype(
            jnp.bfloat16
        )
        saved = (normed, recip_rms, normed_low, query_rows, key_rows, value_rows,
                 attn_probs, probs_low, flat_mixed)
        return rows_out, saved

    def backward_pass(grad_in, saved):
        (normed, recip_rms, normed_low, query_rows, key_rows, value_rows,
         attn_probs, probs_low, flat_mixed) = saved
        grad_mixed = (
            jnp.dot(grad_in, out_local, preferred_element_type=jnp.float32)
            .astype(jnp.bfloat16)
            .reshape(seq_len, groups, GROUP, HD)
        )
        grad_query, grad_key, grad_value = attend_back(
            query_rows, key_rows, value_rows, attn_probs, probs_low, grad_mixed
        )
        grad_proj = jnp.concatenate(
            [
                grad_query.astype(jnp.bfloat16),
                grad_key.astype(jnp.bfloat16)[:, :, None],
                grad_value.astype(jnp.bfloat16)[:, :, None],
            ],
            axis=2,
        ).reshape(seq_len, proj_cols)
        partial_rows = lax.dot_general(
            qkv_local, grad_proj, contract_last, preferred_element_type=jnp.float32
        ).T
        grad_rows, offset = tensor_scatter(partial_rows)
        count = grad_rows.shape[0]
        normed_rows = lax.dynamic_slice_in_dim(normed, offset, count, 0)
        recip_rows = lax.dynamic_slice_in_dim(recip_rms, offset, count, 0)
        grad_in_rows = lax.dynamic_slice_in_dim(grad_in, offset, count, 0)
        grad_float = grad_rows.astype(jnp.float32)
        scaled = grad_float * gain_row
        grad_norm_in = recip_rows * (
            scaled - normed_rows * jnp.mean(scaled * normed_rows, axis=-1, keepdims=True)
        )
        rows_out = (grad_in_rows.astype(jnp.float32) + grad_norm_in).astype(jnp.bfloat16)
        gain_part = jnp.sum(grad_float * normed_rows, axis=0)
        return rows_out, (grad_proj, gain_part)

    incoming = jnp.zeros_like(tokens_local)
    for turn in range(sections):
        block_in = jnp.where(section_index == 0, tokens_local, incoming)
        rows_out, saved = forward_pass(block_in)
        if turn < sections - 1:
            incoming = tensor_gather(pass_section(rows_out, 1), relay_flip())

    incoming = jnp.zeros_like(grads_local)
    for turn in range(sections):
        grad_in = jnp.where(section_index == sections - 1, grads_local, incoming)
        rows_out, (grad_proj, gain_part) = backward_pass(grad_in, saved)
        if turn < sections - 1:
            incoming = tensor_gather(pass_section(rows_out, -1), relay_flip())

    normed_low = saved[2]
    flat_mixed = saved[8]
    seqs = lax.axis_size("dp")
    slice_width = model_width // seqs
    mixed_rows = lax.all_gather(flat_mixed, "dp", axis=0, tiled=True)
    gain_rows = 8
    gain_seq = axis_total(gain_part, "tensor")
    gain_block = jnp.zeros((gain_rows, model_width), jnp.bfloat16).at[0].set(gain_seq.astype(jnp.bfloat16))
    block_rows = 2 * seq_len + gain_rows
    both_cols = lax.all_to_all(
        jnp.concatenate([normed_low, grad_in, gain_block], axis=0), "dp", 1, 0, tiled=True
    ).reshape(seqs, block_rows, slice_width)
    normed_cols = both_cols[:, :seq_len].reshape(seqs * seq_len, slice_width)
    grad_cols = both_cols[:, seq_len : 2 * seq_len].reshape(seqs * seq_len, slice_width)
    gain_slices = both_cols[:, 2 * seq_len].astype(jnp.float32)
    dproj_rows = lax.all_gather(grad_proj, "dp", axis=0, tiled=True)
    qkv_result = lax.dot_general(
        normed_cols, dproj_rows, contract_rows, preferred_element_type=jnp.float32
    )[None]
    out_result = lax.dot_general(
        grad_cols, mixed_rows, contract_rows, preferred_element_type=jnp.float32
    )[None]
    gain_result = jnp.sum(gain_slices, axis=0)[None]
    return (qkv_result, out_result, gain_result)


def solution(mesh):
    in_specs = (
        P("dp", None, None),
        P("pipe", None),
        P("pipe", "dp", "tensor"),
        P("pipe", "dp", "tensor"),
        P("dp", None, None),
    )
    out_specs = (P("pipe", "dp", "tensor"), P("pipe", "dp", "tensor"), P("pipe", "dp"))
    return jax.shard_map(shards, mesh=mesh, in_specs=in_specs, out_specs=out_specs, check_vma=False)
```

```python
import jax
import jax.numpy as jnp
from jax import lax
from jax.sharding import PartitionSpec as P

HD = 128
GROUP = 4
BLOCK = 32


EPSILON = 1e-05
HIGH = lax.Precision.HIGHEST


def from_behind(value, axis, steps):
    count = lax.axis_size(axis)
    leading, last = (max(0, -steps), min(count, count - steps))
    return lax.ppermute(value, axis, [(source, source + steps) for source in range(leading, last)])


def norm_parts(block_rows, gain_row):
    values = block_rows.astype(jnp.float32)
    recip_rms = lax.rsqrt(jnp.mean(values * values, axis=-1, keepdims=True) + EPSILON)
    normed = values * recip_rms
    return (normed, recip_rms, (normed * gain_row).astype(jnp.bfloat16))


def attend(query_rows, key_rows, value_rows, query_pos, key_pos):
    score_scale = query_rows.shape[-1] ** (-0.5)
    scores = (
        jnp.einsum("rgjd,cgd->gjrc", query_rows, key_rows, preferred_element_type=jnp.float32)
        * score_scale
    )
    allowed = key_pos[None, :] <= query_pos[:, None]
    scores = jnp.where(allowed, scores, -jnp.inf)
    row_max = jnp.max(scores, axis=-1, keepdims=True)
    raised = jnp.exp(scores - row_max)
    attn_probs = raised / jnp.sum(raised, axis=-1, keepdims=True)
    probs_low = attn_probs.astype(jnp.bfloat16)
    mixed_rows = jnp.einsum(
        "gjrc,cgd->rgjd", probs_low, value_rows, preferred_element_type=jnp.float32
    )
    return (attn_probs, probs_low, mixed_rows.astype(jnp.bfloat16))


def attend_back(query_rows, key_rows, value_rows, attn_probs, probs_low, grad_mixed):
    score_scale = query_rows.shape[-1] ** (-0.5)
    grad_low = jnp.einsum(
        "rgjd,cgd->gjrc", grad_mixed, value_rows, preferred_element_type=jnp.float32
    )
    inner_sum = jnp.sum(attn_probs * grad_low, axis=-1, keepdims=True)
    grad_score = attn_probs * (grad_low - inner_sum) * score_scale
    grad_query = jnp.einsum(
        "gjrc,cgd->rgjd", grad_score, key_rows.astype(jnp.float32), precision=HIGH
    )
    grad_key = jnp.einsum(
        "gjrc,rgjd->cgd", grad_score, query_rows.astype(jnp.float32), precision=HIGH
    )
    grad_value = jnp.einsum(
        "gjrc,rgjd->cgd", probs_low, grad_mixed, preferred_element_type=jnp.float32
    )
    return (grad_query, grad_key, grad_value)


def exchange(value, axis, mask):
    count = lax.axis_size(axis)
    return lax.ppermute(value, axis, [(source, source ^ mask) for source in range(count)])


def tensor_scatter(partial_rows):
    count = lax.axis_size("tensor")
    member = lax.axis_index("tensor")
    values = partial_rows.astype(jnp.bfloat16)
    offset = 0
    mask = 1
    while mask < count:
        bit = (member // mask) % 2
        half = values.shape[0] // 2
        keep = lax.dynamic_slice_in_dim(values, bit * half, half, 0)
        give = lax.dynamic_slice_in_dim(values, (1 - bit) * half, half, 0)
        values = (
            keep.astype(jnp.float32) + exchange(give, "tensor", mask).astype(jnp.float32)
        ).astype(jnp.bfloat16)
        offset = offset + bit * half
        mask *= 2
    return values, offset


def tensor_gather(block, flip=0):
    count = lax.axis_size("tensor")
    member = lax.axis_index("tensor")
    values = block
    mask = count // 2
    while mask >= 1:
        bit = ((member ^ flip) // mask) % 2
        other = exchange(values, "tensor", mask)
        values = jnp.where(
            bit == 0,
            jnp.concatenate([values, other], axis=0),
            jnp.concatenate([other, values], axis=0),
        )
        mask //= 2
    return values


def tensor_total(vector):
    count = lax.axis_size("tensor")
    mask = 1
    while mask < count:
        vector = vector + exchange(vector, "tensor", mask)
        mask *= 2
    return vector


def group_total(vector, axis, stride, size):
    count = lax.axis_size(axis)
    member = lax.axis_index(axis)
    digit = (member // stride) % size

    def moved(source, shift):
        source_digit = (source // stride) % size
        return source + ((source_digit + shift) % size - source_digit) * stride

    received = [vector] + [
        lax.ppermute(vector, axis, [(source, moved(source, shift)) for source in range(count)])
        for shift in range(1, size)
    ]
    stacked = jnp.stack(received)
    ordered = [stacked[(digit - j) % size] for j in range(size)]
    while len(ordered) > 1:
        ordered = [ordered[i] + ordered[i + 1] for i in range(0, len(ordered), 2)]
    return ordered[0]


def axis_total(vector, axis):
    count = lax.axis_size(axis)
    stride = 1
    while stride < count:
        size = min(4, count // stride)
        vector = group_total(vector, axis, stride, size)
        stride *= size
    return vector


def relay_flip():
    return lax.axis_size("tensor") // 2


def pass_section(block_value, offset):
    sections = lax.axis_size("pipe")
    members = lax.axis_size("tensor")
    flip = relay_flip()
    pairs = [
        (source * members + member, (source + offset) * members + (member ^ flip))
        for source in range(sections)
        if 0 <= source + offset < sections
        for member in range(members)
    ]
    return lax.ppermute(block_value, ("pipe", "tensor"), pairs)


def keep_active(active, fresh_state, old_state):
    return jax.tree.map(lambda fresh, old: jnp.where(active, fresh, old), fresh_state, old_state)


def shards(tokens, norm_gains, qkv_weight, out_weight, cotangent):
    sections = lax.axis_size("pipe")
    section_index = lax.axis_index("pipe")
    qkv_cols = qkv_weight.shape[2]
    joined = jnp.concatenate([qkv_weight, out_weight], axis=2)
    joined_full = lax.all_gather(joined, "dp", axis=1, tiled=True)[0]
    qkv_local = joined_full[:, :qkv_cols]
    out_local = joined_full[:, qkv_cols:]
    gain_row = norm_gains[0]
    tokens_local = tokens[0]
    grads_local = cotangent[0]
    seq_len = tokens_local.shape[0]
    model_width = tokens_local.shape[1]
    proj_cols = qkv_local.shape[1]
    groups = proj_cols // ((GROUP + 2) * HD)
    head_cols = groups * GROUP * HD
    positions = jnp.arange(seq_len)
    contract_last = (((1,), (1,)), ((), ()))
    contract_rows = (((0,), (0,)), ((), ()))

    def forward_pass(block_in):
        normed, recip_rms, normed_low = norm_parts(block_in, gain_row)
        projected = lax.optimization_barrier(
            jnp.dot(normed_low, qkv_local, preferred_element_type=jnp.float32)
        ).reshape(seq_len, groups, GROUP + 2, HD)
        query_rows = projected[:, :, :GROUP].astype(jnp.bfloat16)
        key_rows = projected[:, :, GROUP].astype(jnp.bfloat16)
        value_rows = projected[:, :, GROUP + 1].astype(jnp.bfloat16)
        attn_probs, probs_low, mixed_rows = attend(
            query_rows, key_rows, value_rows, positions, positions
        )
        flat_mixed = mixed_rows.reshape(seq_len, head_cols)
        partial_rows = lax.dot_general(
            flat_mixed, out_local, contract_last, preferred_element_type=jnp.float32
        )
        summed_rows, offset = tensor_scatter(partial_rows)
        rows_in = lax.dynamic_slice_in_dim(block_in, offset, summed_rows.shape[0], 0)
        rows_out = (rows_in.astype(jnp.float32) + summed_rows.astype(jnp.float32)).astype(
            jnp.bfloat16
        )
        saved = (normed, recip_rms, normed_low, query_rows, key_rows, value_rows,
                 attn_probs, probs_low, flat_mixed)
        return rows_out, saved

    def backward_pass(grad_in, saved):
        (normed, recip_rms, normed_low, query_rows, key_rows, value_rows,
         attn_probs, probs_low, flat_mixed) = saved
        grad_mixed = (
            jnp.dot(grad_in, out_local, preferred_element_type=jnp.float32)
            .astype(jnp.bfloat16)
            .reshape(seq_len, groups, GROUP, HD)
        )
        grad_query, grad_key, grad_value = attend_back(
            query_rows, key_rows, value_rows, attn_probs, probs_low, grad_mixed
        )
        grad_proj = jnp.concatenate(
            [
                grad_query.astype(jnp.bfloat16),
                grad_key.astype(jnp.bfloat16)[:, :, None],
                grad_value.astype(jnp.bfloat16)[:, :, None],
            ],
            axis=2,
        ).reshape(seq_len, proj_cols)
        partial_rows = lax.dot_general(
            grad_proj, qkv_local, contract_last, preferred_element_type=jnp.float32
        )
        grad_rows, offset = tensor_scatter(partial_rows)
        count = grad_rows.shape[0]
        normed_rows = lax.dynamic_slice_in_dim(normed, offset, count, 0)
        recip_rows = lax.dynamic_slice_in_dim(recip_rms, offset, count, 0)
        grad_in_rows = lax.dynamic_slice_in_dim(grad_in, offset, count, 0)
        grad_float = grad_rows.astype(jnp.float32)
        scaled = grad_float * gain_row
        grad_norm_in = recip_rows * (
            scaled - normed_rows * jnp.mean(scaled * normed_rows, axis=-1, keepdims=True)
        )
        rows_out = (grad_in_rows.astype(jnp.float32) + grad_norm_in).astype(jnp.bfloat16)
        gain_part = jnp.sum(grad_float * normed_rows, axis=0)
        return rows_out, (grad_proj, gain_part)

    incoming = jnp.zeros_like(tokens_local)
    for turn in range(sections):
        block_in = jnp.where(section_index == 0, tokens_local, incoming)
        rows_out, saved = forward_pass(block_in)
        if turn < sections - 1:
            incoming = tensor_gather(pass_section(rows_out, 1), relay_flip())

    incoming = jnp.zeros_like(grads_local)
    for turn in range(sections):
        grad_in = jnp.where(section_index == sections - 1, grads_local, incoming)
        rows_out, (grad_proj, gain_part) = backward_pass(grad_in, saved)
        if turn < sections - 1:
            incoming = tensor_gather(pass_section(rows_out, -1), relay_flip())

    normed_low = saved[2]
    flat_mixed = saved[8]
    seqs = lax.axis_size("dp")
    slice_width = model_width // seqs
    mixed_rows = lax.all_gather(flat_mixed, "dp", axis=0, tiled=True)
    gain_rows = 8
    gain_seq = axis_total(gain_part, "tensor")
    gain_block = jnp.zeros((gain_rows, model_width), jnp.bfloat16).at[0].set(gain_seq.astype(jnp.bfloat16))
    block_rows = 2 * seq_len + gain_rows
    both_cols = lax.all_to_all(
        jnp.concatenate([normed_low, grad_in, gain_block], axis=0), "dp", 1, 0, tiled=True
    ).reshape(seqs, block_rows, slice_width)
    normed_cols = both_cols[:, :seq_len].reshape(seqs * seq_len, slice_width)
    grad_cols = both_cols[:, seq_len : 2 * seq_len].reshape(seqs * seq_len, slice_width)
    gain_slices = both_cols[:, 2 * seq_len].astype(jnp.float32)
    dproj_rows = lax.all_gather(grad_proj, "dp", axis=0, tiled=True)
    qkv_result = lax.dot_general(
        normed_cols, dproj_rows, contract_rows, preferred_element_type=jnp.float32
    )[None]
    out_result = lax.dot_general(
        grad_cols, mixed_rows, contract_rows, preferred_element_type=jnp.float32
    )[None]
    gain_result = jnp.sum(gain_slices, axis=0)[None]
    return (qkv_result, out_result, gain_result)


def solution(mesh):
    in_specs = (
        P("dp", None, None),
        P("pipe", None),
        P("pipe", "dp", "tensor"),
        P("pipe", "dp", "tensor"),
        P("dp", None, None),
    )
    out_specs = (P("pipe", "dp", "tensor"), P("pipe", "dp", "tensor"), P("pipe", "dp"))
    return jax.shard_map(shards, mesh=mesh, in_specs=in_specs, out_specs=out_specs, check_vma=False)
```
